128 devices in a mesh: dp: 4 (over z_lo, core), tensor: 32 (over y, x, z_hi).
Axes of the slice: x: 4, y: 4, z: 4 (z_hi: 2, z_lo: 2; z = z_hi * 2 + z_lo), core: 2. Of those that a mesh axis runs over, the one named last changes fastest.
Arguments:
- stream: bfloat16 [6144, 2560], P(('dp', 'tensor')), may hold values from -26 to 26
- lengths: int32 [4, 6], P('dp'), may hold values from 16 to 768, as said below
- page_table: int32 [384], P('dp'), may hold values from 0 to 383, as said below
- request_prompt: int32 [64], P('dp'), may hold values from 0 to 23
- attn_gain: bfloat16 [2560], replicated, may hold values from 0.099609375 to 1.8984375
- query_gain: bfloat16 [128], replicated, may hold values from 0.5 to 10, as said below
- key_gain: bfloat16 [128], replicated, may hold values from 0.5 to 10, as said below
- mlp_gain: bfloat16 [2560], replicated, may hold values from 0.099609375 to 1.8984375
- w_query: bfloat16 [2560, 4096], P(None, 'tensor'), may hold values from -0.125 to 0.125
- key_value_weight: bfloat16 [2560, 2048], P(None, 'tensor'), may hold values from -0.125 to 0.125
- w_out: bfloat16 [4096, 2560], P('tensor'), may hold values from -0.5 to 0.5
- w_gate: bfloat16 [2560, 9728], P(None, 'tensor'), may hold values from -0.125 to 0.125
- w_up: bfloat16 [2560, 9728], P(None, 'tensor'), may hold values from -0.125 to 0.125
- w_down: bfloat16 [9728, 2560], P('tensor'), may hold values from -0.0625 to 0.0625
Outputs:
- layer_out: bfloat16 [6144, 2560], P(('dp', 'tensor'))
- paged_key_value_cache: bfloat16 [384, 16, 2048], P('dp', None, 'tensor')
- request_state: bfloat16 [64, 2560], P('dp', 'tensor')
The draws below stay inside these ranges and needn't reach their ends.
Inputs may be any that keep to these rules, and one draw needn't show every extreme that they name: Every length is a multiple of 16; each batch's lengths add up to 1536, and the largest length of each batch is exactly 768. page_table is a permutation of all global slots; slot v belongs to owner v // 96, and each batch writes exactly 24 pages to each owner. `query_gain`: positive gains. `key_gain`: positive gains.
All inputs are finite; a program needn't handle non-finite values.
Results may differ from the reference program's by a relative error of at most 0.02.
The reference program's roundings to bfloat16 on the way count: a program that leaves them out, or rounds other values in their place, can miss the bound.
Values may be sent and summed in bfloat16 or wider, within the bound.
No kernel may reach another device: no remote copies, remote signals or barrier semaphores. Data moves between devices by JAX's collectives and lax.ppermute only.
A program may use at most 128 MiB of HBM per device.

```python
import math
import jax
import jax.numpy as jnp
from jax import lax

MODEL_WIDTH = 2560
QUERY_HEADS = 32
KEY_VALUE_HEADS = 8
HEAD_SIZE = 128
FF = 9728
PAGE_TOKENS = 16
NPROMPT = 6
NREQ = 16
BATCH_TOKENS = 1536
BATCH_COUNT = 4
ROWS = 6144
PAGES_PER_BATCH = 96
CAPP = 24
N_TENSOR = 32


def draw_stream(key, part):
    key = jax.random.fold_in(key, 5)
    base_key, row_key, col_key = jax.random.split(key, 3)
    row_scale = jnp.exp(jax.random.uniform(row_key, (ROWS, 1), minval=math.log(0.3), maxval=math.log(3.0)))
    col_scale = jnp.exp(jax.random.uniform(col_key, (1, MODEL_WIDTH), minval=math.log(0.5), maxval=math.log(2.0)))
    base = jnp.clip(jax.random.normal(base_key, (ROWS, MODEL_WIDTH)), -4.0, 4.0)
    return (base * row_scale * col_scale).astype(jnp.float32).astype(jnp.bfloat16)


def head_gain(key, salt):
    key = jax.random.fold_in(key, salt)
    values = jax.random.uniform(key, (HEAD_SIZE,), minval=0.5, maxval=2.0)
    return values.astype(jnp.float32).astype(jnp.bfloat16)


def draw_query_gain(key, part):
    return head_gain(key, 17)


def draw_key_gain(key, part):
    return head_gain(key, 29)


def draw_lengths(key, part):
    key = jax.random.fold_in(key, 11)

    def one_batch(batch_key):
        cut_key, order_key = jax.random.split(batch_key)
        longest_pages = PAGES_PER_BATCH // 2
        spare = PAGES_PER_BATCH - longest_pages - (NPROMPT - 1)
        cuts = jnp.sort(jax.random.randint(cut_key, (NPROMPT - 2,), 0, spare + 1))
        edges = jnp.concatenate([jnp.zeros((1,), jnp.int32), cuts.astype(jnp.int32), jnp.full((1,), spare, jnp.int32)])
        others = edges[1:] - edges[:-1] + 1
        counts = jnp.concatenate([jnp.full((1,), longest_pages, jnp.int32), others])
        return (jax.random.permutation(order_key, counts) * PAGE_TOKENS).astype(jnp.int32)
    return jax.vmap(one_batch)(jax.random.split(key, BATCH_COUNT))


def draw_page_table(key, part):
    key = jax.random.fold_in(key, 23)
    order_key, slot_key = jax.random.split(key)
    orders = jax.vmap(lambda one_key: jax.random.permutation(one_key, PAGES_PER_BATCH))(jax.random.split(order_key, BATCH_COUNT)).astype(jnp.int32)
    owner_slots = jax.vmap(lambda one_key: jax.random.permutation(one_key, PAGES_PER_BATCH))(jax.random.split(slot_key, BATCH_COUNT)).astype(jnp.int32)
    position = jnp.arange(PAGES_PER_BATCH, dtype=jnp.int32)
    owners = position // CAPP
    within = position % CAPP
    sources = jnp.arange(BATCH_COUNT, dtype=jnp.int32)[:, None]
    dest = owners[None, :] * PAGES_PER_BATCH + owner_slots[owners[None, :], sources * CAPP + within[None, :]]
    table = jnp.zeros((BATCH_COUNT, PAGES_PER_BATCH), jnp.int32).at[jnp.broadcast_to(sources, (BATCH_COUNT, PAGES_PER_BATCH)), orders].set(dest.astype(jnp.int32))
    return table.reshape(BATCH_COUNT * PAGES_PER_BATCH)


def with_ends(array, rng, smallest, top_value):
    dims = array.shape
    place = [jax.random.randint(jax.random.fold_in(rng, axis), (), 0, dims[axis]) for axis in range(len(dims))]
    array = array.at[tuple(place)].set(smallest)
    longest = dims.index(max(dims))
    place[longest] = (place[longest] + 1) % dims[longest]
    return array.at[tuple(place)].set(top_value)


def block_levels(rng, extent, pieces, least, top_value):
    factor_of, own = 1.0, jax.random.fold_in(rng, 6)
    for dim, blocks in pieces:
        heights = jnp.exp(jax.random.uniform(jax.random.fold_in(own, dim), (blocks,), jnp.float32, least / len(pieces), top_value / len(pieces)))
        factor_of = factor_of * jnp.repeat(heights, extent[dim] // blocks).reshape([-1 if axis == dim else 1 for axis in range(len(extent))])
    return factor_of


def centred(rng, shape, width, bound, cuts=(), kind=jnp.bfloat16):
    level = block_levels(rng, shape, cuts, -0.22, 0.18) if cuts else 1.0
    array = jax.random.normal(rng, shape, jnp.float32) * width * level
    return jnp.minimum(jnp.maximum(array, -bound), bound).astype(kind)


def setup_inputs(seed: int = 0) -> dict:
    streams_of = jax.random.split(jax.random.key(seed), 15)
    return {
        "stream": draw_stream(jax.random.fold_in(streams_of[14], 71), 0),
        "lengths": draw_lengths(jax.random.fold_in(streams_of[14], 71), 0),
        "page_table": draw_page_table(jax.random.fold_in(streams_of[14], 71), 0),
        "request_prompt": with_ends(jax.random.randint(streams_of[3], (BATCH_COUNT * NREQ,), 0, BATCH_COUNT * NPROMPT), jax.random.fold_in(streams_of[3], 1), 0, (BATCH_COUNT * NPROMPT) - 1).astype(jnp.int32),
        "attn_gain": jnp.clip(1.0 + 0.18 * jax.random.normal(streams_of[4], (MODEL_WIDTH,), jnp.float32), 0.099609375, 1.8984375).astype(jnp.bfloat16),
        "query_gain": draw_query_gain(jax.random.fold_in(streams_of[14], 71), 0),
        "key_gain": draw_key_gain(jax.random.fold_in(streams_of[14], 71), 0),
        "mlp_gain": jnp.clip(1.0 + 0.18 * jax.random.normal(streams_of[7], (MODEL_WIDTH,), jnp.float32), 0.099609375, 1.8984375).astype(jnp.bfloat16),
        "w_query": centred(streams_of[8], (MODEL_WIDTH, QUERY_HEADS * HEAD_SIZE), MODEL_WIDTH ** -0.5, 0.125, ((1, 32),)),
        "key_value_weight": centred(streams_of[9], (MODEL_WIDTH, 2 * KEY_VALUE_HEADS * HEAD_SIZE), MODEL_WIDTH ** -0.5, 0.125, ((1, 32),)),
        "w_out": centred(streams_of[10], (QUERY_HEADS * HEAD_SIZE, MODEL_WIDTH), HEAD_SIZE ** -0.5, 0.5, ((0, 32),)),
        "w_gate": centred(streams_of[11], (MODEL_WIDTH, FF), MODEL_WIDTH ** -0.5, 0.125, ((1, 32),)),
        "w_up": centred(streams_of[12], (MODEL_WIDTH, FF), MODEL_WIDTH ** -0.5, 0.125, ((1, 32),)),
        "w_down": centred(streams_of[13], (FF, MODEL_WIDTH), FF ** -0.5, 0.0625, ((0, 32),)),
    }


epsilon = 1e-06
rope_base = 1000000.0

def row_norm(inputs, gain):
    inputs = inputs.astype(jnp.float32)
    scale = lax.rsqrt(lax.optimization_barrier(jnp.mean(inputs * inputs, axis=-1, keepdims=True)) + epsilon)
    return inputs * scale * gain.astype(jnp.float32)

def rotate(inputs, position):
    half_dim = inputs.shape[-1] // 2
    frequency = rope_base ** (-2.0 * jnp.arange(half_dim, dtype=jnp.float32) / inputs.shape[-1])
    angles = position.astype(jnp.float32)[:, None] * frequency[None, :]
    cosine = jnp.cos(angles)[:, None, :]
    sine_part = jnp.sin(angles)[:, None, :]
    front = inputs[..., :half_dim]
    second = inputs[..., half_dim:]
    return jnp.concatenate([front * cosine - second * sine_part, second * cosine + front * sine_part], axis=-1)

def prompt_layout(lengths_row, token_count):
    lengths_row = lengths_row.astype(jnp.int32)
    prompt_ends = jnp.cumsum(lengths_row).astype(jnp.int32)
    prompt_starts = (prompt_ends - lengths_row).astype(jnp.int32)
    row_ids = jnp.arange(token_count, dtype=jnp.int32)
    prompt = lax.optimization_barrier(jnp.sum((row_ids[:, None] >= prompt_ends[None, :]).astype(jnp.int32), axis=1)).astype(jnp.int32)
    inside = (row_ids[:, None] >= prompt_starts[None, :]) & (row_ids[:, None] < prompt_ends[None, :])
    offset = lax.optimization_barrier(jnp.sum(jnp.where(inside, prompt_starts[None, :], 0), axis=1)).astype(jnp.int32)
    return (prompt, (row_ids - offset).astype(jnp.int32), prompt_starts, prompt_ends)

def block_sum(left, right, block_count):
    width_block = left.shape[1] // block_count

    def add_block(block_id, summed):
        portion = lax.dynamic_slice_in_dim(left, block_id * width_block, width_block, 1)
        weights = lax.dynamic_slice_in_dim(right, block_id * width_block, width_block, 0)
        partial_value = jnp.dot(portion, weights, preferred_element_type=jnp.float32).astype(jnp.bfloat16)
        partial_value = lax.optimization_barrier(partial_value)
        return summed + partial_value.astype(jnp.float32)
    start_sum = jnp.zeros((left.shape[0], right.shape[1]), jnp.float32)
    return lax.fori_loop(jnp.int32(0), jnp.int32(block_count), add_block, start_sum)

def reference(stream, lengths, page_table, request_prompt, attn_gain, query_gain, key_gain, mlp_gain, w_query, key_value_weight, w_out, w_gate, w_up, w_down):
    queries_per_key_value = QUERY_HEADS // KEY_VALUE_HEADS
    outputs = []
    last_rows = []
    paged_key_value_cache = jnp.zeros((BATCH_COUNT * PAGES_PER_BATCH, PAGE_TOKENS, 2 * KEY_VALUE_HEADS * HEAD_SIZE), jnp.bfloat16)
    token_ids = jnp.arange(BATCH_TOKENS, dtype=jnp.int32)
    for group_id in range(BATCH_COUNT):
        rows_in = stream[group_id * BATCH_TOKENS:(group_id + 1) * BATCH_TOKENS]
        prompt, position, prompt_starts, prompt_ends = prompt_layout(lengths[group_id], BATCH_TOKENS)
        normalized_rows = row_norm(rows_in, attn_gain).astype(jnp.bfloat16)
        queries = jnp.dot(normalized_rows, w_query, preferred_element_type=jnp.float32).reshape(BATCH_TOKENS, QUERY_HEADS, HEAD_SIZE)
        key_value_rows = jnp.dot(normalized_rows, key_value_weight, preferred_element_type=jnp.float32).astype(jnp.bfloat16).reshape(BATCH_TOKENS, KEY_VALUE_HEADS, 2, HEAD_SIZE)
        q_rot = rotate(row_norm(queries, query_gain), position).astype(jnp.bfloat16)
        rotated_key = rotate(row_norm(key_value_rows[:, :, 0, :], key_gain), position).astype(jnp.bfloat16)
        value_matrix_rows = key_value_rows[:, :, 1, :]
        allowed = (prompt[:, None] == prompt[None, :]) & (token_ids[:, None] >= token_ids[None, :])
        heads_out = []
        for key_value_head in range(KEY_VALUE_HEADS):
            q_group = q_rot[:, key_value_head * queries_per_key_value:(key_value_head + 1) * queries_per_key_value, :].astype(jnp.float32)
            key_head = rotated_key[:, key_value_head, :].astype(jnp.float32)
            scores = jnp.einsum('qhd,kd->hqk', q_group, key_head, precision=lax.Precision.HIGHEST) / math.sqrt(HEAD_SIZE)
            peak = lax.optimization_barrier(jnp.max(jnp.where(allowed[None], scores, -jnp.inf), axis=2, keepdims=True))
            weight = jnp.where(allowed[None], jnp.exp(scores - peak), 0.0)
            total_weight = lax.optimization_barrier(jnp.sum(weight, axis=2, keepdims=True))
            probs = lax.optimization_barrier(weight.astype(jnp.bfloat16)).astype(jnp.float32)
            mixed = jnp.einsum('hqk,kd->qhd', probs, value_matrix_rows[:, key_value_head, :].astype(jnp.float32), precision=lax.Precision.HIGHEST)
            heads_out.append((mixed / jnp.transpose(total_weight, (1, 0, 2))).astype(jnp.bfloat16))
        attn = jnp.concatenate(heads_out, axis=1).reshape(BATCH_TOKENS, QUERY_HEADS * HEAD_SIZE)
        attn_sum = block_sum(attn, w_out, N_TENSOR)
        resid = (rows_in.astype(jnp.float32) + attn_sum).astype(jnp.bfloat16)
        mlp_normed = row_norm(resid, mlp_gain).astype(jnp.bfloat16)
        gate_rows = jnp.dot(mlp_normed, w_gate, preferred_element_type=jnp.float32)
        upward = jnp.dot(mlp_normed, w_up, preferred_element_type=jnp.float32)
        hidden = (jax.nn.silu(gate_rows) * upward).astype(jnp.bfloat16)
        mlp_sum = block_sum(hidden, w_down, N_TENSOR)
        layer_rows = (resid.astype(jnp.float32) + mlp_sum).astype(jnp.bfloat16)
        outputs.append(layer_rows)
        cache_pages = jnp.stack([rotated_key, value_matrix_rows], axis=2).reshape(PAGES_PER_BATCH, PAGE_TOKENS, 2 * KEY_VALUE_HEADS * HEAD_SIZE)
        paged_key_value_cache = paged_key_value_cache.at[page_table[group_id * PAGES_PER_BATCH:(group_id + 1) * PAGES_PER_BATCH]].set(cache_pages)
        last_rows.append(layer_rows[prompt_ends - 1])
    layer_out = jnp.concatenate(outputs, axis=0)
    table = jnp.concatenate(last_rows, axis=0)
    request_state = table[request_prompt]
    return (layer_out, paged_key_value_cache, request_state)
```

```python
import math

import jax
import jax.numpy as jnp
from jax import lax
from jax.sharding import PartitionSpec as P

KEY_VALUE_HEADS = 8
HEAD_SIZE = 128
PAGE_TOKENS = 16


epsilon = 1e-06
rope_base = 1000000.0


def partner_2(value, axis, bit):
    mask = 2**bit
    pairs = [(source, source ^ mask) for source in range(lax.axis_size(axis))]
    return lax.ppermute(value, axis, pairs)


def scatter_sum(partial, parts):
    pieces = partial.reshape((parts, partial.shape[0] // parts) + partial.shape[1:])
    got = lax.all_to_all(pieces, "tensor", 0, 0, tiled=True)
    return jnp.sum(got.astype(jnp.float32), axis=0)


def row_norm(inputs, gain):
    inputs = inputs.astype(jnp.float32)
    scale = lax.rsqrt(jnp.mean(inputs * inputs, axis=-1, keepdims=True) + epsilon)
    return inputs * scale * gain.astype(jnp.float32)


def rotate(inputs, position):
    half_dim = inputs.shape[-1] // 2
    frequency = rope_base ** (-2.0 * jnp.arange(half_dim, dtype=jnp.float32) / inputs.shape[-1])
    angles = position.astype(jnp.float32)[:, None] * frequency[None, :]
    cosine = jnp.cos(angles)[:, None, :]
    sine_part = jnp.sin(angles)[:, None, :]
    front = inputs[..., :half_dim]
    second = inputs[..., half_dim:]
    return jnp.concatenate(
        [front * cosine - second * sine_part, second * cosine + front * sine_part], axis=-1
    )


def prompt_layout(lengths_row, token_count):
    prompt_ends = jnp.cumsum(lengths_row)
    prompt_starts = prompt_ends - lengths_row
    row_ids = jnp.arange(token_count, dtype=jnp.int32)
    prompt = jnp.sum((row_ids[:, None] >= prompt_ends[None, :]).astype(jnp.int32), axis=1)
    inside = (row_ids[:, None] >= prompt_starts[None, :]) & (
        row_ids[:, None] < prompt_ends[None, :]
    )
    offset = jnp.sum(jnp.where(inside, prompt_starts[None, :], 0), axis=1)
    return (prompt, row_ids - offset, prompt_starts, prompt_ends)


def per_device(
    stream,
    lengths,
    page_table,
    request_prompt,
    attn_gain,
    query_gain,
    key_gain,
    mlp_gain,
    w_query,
    key_value_weight,
    w_out,
    w_gate,
    w_up,
    w_down,
):
    tok_dev = stream.shape[0]
    tensor_element_count = lax.axis_size("tensor")
    token_count = tok_dev * tensor_element_count
    my_index = lax.axis_index("tensor")
    heads_dev = w_query.shape[1] // HEAD_SIZE
    query_cols = heads_dev * HEAD_SIZE
    prompt, position, prompt_starts, prompt_ends = prompt_layout(lengths[0], token_count)
    portion = lax.all_gather(
        row_norm(stream, attn_gain).astype(jnp.bfloat16), "tensor", axis=0, tiled=True
    )
    joined = jnp.concatenate(
        [
            jnp.dot(portion, w_query, preferred_element_type=jnp.float32),
            jnp.dot(portion, key_value_weight, preferred_element_type=jnp.float32),
        ],
        axis=1,
    )
    queries = joined[:, :query_cols].reshape(token_count, heads_dev, HEAD_SIZE)
    kv_part = joined[:, query_cols:].astype(jnp.bfloat16)
    key_value_group = tensor_element_count // KEY_VALUE_HEADS
    for bit_id in range(key_value_group.bit_length() - 1):
        partner = partner_2(kv_part, "tensor", bit_id)
        upper_half = my_index // 2**bit_id % 2
        kv_part = jnp.where(
            upper_half == 1,
            jnp.concatenate([partner, kv_part], axis=1),
            jnp.concatenate([kv_part, partner], axis=1),
        )
    key_flat = rotate(row_norm(kv_part[:, None, :HEAD_SIZE], key_gain), position).astype(
        jnp.bfloat16
    )[:, 0, :]
    value_matrix_rows = kv_part[:, HEAD_SIZE:]
    q_rot = rotate(row_norm(queries, query_gain), position).astype(jnp.bfloat16)
    piece_cols = key_value_weight.shape[1]
    head_rows = jnp.concatenate([key_flat, value_matrix_rows], axis=1)
    own_cols = lax.dynamic_slice_in_dim(
        head_rows, my_index % key_value_group * piece_cols, piece_cols, 1
    )
    page_count = token_count // PAGE_TOKENS
    page_rows = own_cols.reshape(page_count, PAGE_TOKENS, piece_cols)
    group_count = lax.axis_size("dp")
    capacity = page_count // group_count
    owners = page_table // page_count
    slot_ids = page_table % page_count
    hits = (owners[:, None] == jnp.arange(group_count, dtype=jnp.int32)[None, :]).astype(jnp.int32)
    order_in = jnp.sum((jnp.cumsum(hits, axis=0) - hits) * hits, axis=1)
    buffer_pos = owners * capacity + order_in
    source = (
        jnp.zeros((page_count,), jnp.int32)
        .at[buffer_pos]
        .set(jnp.arange(page_count, dtype=jnp.int32))
    )
    send_pages = page_rows[source].reshape(group_count, capacity, PAGE_TOKENS, piece_cols)
    send_slots = slot_ids[source].reshape(group_count, capacity)
    got_pages, got_slots = (
        lax.all_to_all(send_pages, "dp", split_axis=0, concat_axis=0, tiled=True),
        lax.all_to_all(send_slots, "dp", split_axis=0, concat_axis=0, tiled=True),
    )
    paged_key_value_cache = (
        jnp.zeros((page_count, PAGE_TOKENS, piece_cols), jnp.bfloat16)
        .at[got_slots.reshape(-1)]
        .set(got_pages.reshape(page_count, PAGE_TOKENS, piece_cols))
    )
    block_rows = min(512, token_count)
    block_total = token_count // block_rows
    score_scale = math.sqrt(HEAD_SIZE)
    all_ids = jnp.arange(token_count, dtype=jnp.int32)
    local_ids = jnp.arange(block_rows, dtype=jnp.int32)

    def dense_block(block_index):
        first_row = block_index * block_rows
        q_block = lax.dynamic_slice_in_dim(q_rot, first_row, block_rows, 0)
        q_prompt = lax.dynamic_slice_in_dim(prompt, first_row, block_rows, 0)
        row_ids = first_row + local_ids
        scores = (
            jnp.einsum("qhd,kd->hqk", q_block, key_flat, preferred_element_type=jnp.float32)
            / score_scale
        )
        allowed = ((q_prompt[:, None] == prompt[None, :]) & (row_ids[:, None] >= all_ids[None, :]))[
            None
        ]
        peak = jnp.max(jnp.where(allowed, scores, -jnp.inf), axis=2, keepdims=True)
        weight = jnp.where(allowed, jnp.exp(scores - peak), 0.0)
        total_weight = jnp.sum(weight, axis=2, keepdims=True)
        running = jnp.einsum(
            "hqk,kd->hqd",
            weight.astype(jnp.bfloat16),
            value_matrix_rows,
            preferred_element_type=jnp.float32,
        )
        return (running / total_weight).astype(jnp.bfloat16)

    block_ids = jnp.arange(block_total, dtype=jnp.int32)
    blocks_out = lax.map(dense_block, block_ids)
    attn = jnp.transpose(blocks_out, (0, 2, 1, 3)).reshape(token_count, query_cols)
    attn_sum = scatter_sum(
        jnp.dot(attn, w_out, preferred_element_type=jnp.float32).astype(jnp.bfloat16),
        tensor_element_count,
    )
    resid = (stream.astype(jnp.float32) + attn_sum).astype(jnp.bfloat16)
    portion = lax.all_gather(
        row_norm(resid, mlp_gain).astype(jnp.bfloat16), "tensor", axis=0, tiled=True
    )
    gate_rows = jnp.dot(portion, w_gate, preferred_element_type=jnp.float32)
    upward = jnp.dot(portion, w_up, preferred_element_type=jnp.float32)
    hidden = (jax.nn.silu(gate_rows) * upward).astype(jnp.bfloat16)
    mlp_sum = scatter_sum(
        jnp.dot(hidden, w_down, preferred_element_type=jnp.float32).astype(jnp.bfloat16),
        tensor_element_count,
    )
    layer_out = (resid.astype(jnp.float32) + mlp_sum).astype(jnp.bfloat16)
    my_rows = my_index * tok_dev + jnp.arange(tok_dev, dtype=jnp.int32)
    select = ((prompt_ends - 1)[:, None] == my_rows[None, :]).astype(jnp.bfloat16)
    end_terms = jnp.dot(select, layer_out, preferred_element_type=jnp.float32)
    end_blocks = end_terms.astype(jnp.bfloat16).reshape(
        end_terms.shape[0], tensor_element_count, -1
    )
    end_rows = scatter_sum(jnp.transpose(end_blocks, (1, 0, 2)), tensor_element_count)[0].astype(
        jnp.bfloat16
    )
    table = lax.all_gather(end_rows, "dp", axis=0, tiled=True)
    pick = (request_prompt[:, None] == jnp.arange(table.shape[0], dtype=jnp.int32)[None, :]).astype(
        jnp.bfloat16
    )
    request_state = jnp.dot(pick, table, preferred_element_type=jnp.float32).astype(jnp.bfloat16)
    return (layer_out, paged_key_value_cache, request_state)


def solution(mesh):
    placed = (
        P(("dp", "tensor"), None),
        P("dp", None),
        P("dp"),
        P("dp"),
        P(),
        P(),
        P(),
        P(),
        P(None, "tensor"),
        P(None, "tensor"),
        P("tensor", None),
        P(None, "tensor"),
        P(None, "tensor"),
        P("tensor", None),
    )
    return jax.shard_map(
        per_device,
        mesh=mesh,
        in_specs=placed,
        out_specs=(P(("dp", "tensor"), None), P("dp", None, "tensor"), P("dp", "tensor")),
        check_vma=False,
    )
```

```python
import math

import jax
import jax.numpy as jnp
from jax import lax
from jax.sharding import PartitionSpec as P

KEY_VALUE_HEADS = 8
HEAD_SIZE = 128
PAGE_TOKENS = 16
TENSOR = ("ty", "tx", "tz")
TENSOR_SHAPE = (4, 4, 2)


epsilon = 1e-06
rope_base = 1000000.0


def partner_2(value, axis, bit):
    mask = 2**bit
    pairs = [(source, source ^ mask) for source in range(lax.axis_size(axis))]
    return lax.ppermute(value, axis, pairs)


def scatter_sum(partial, parts):
    pieces = partial.reshape((parts, partial.shape[0] // parts) + partial.shape[1:])
    got = lax.all_to_all(pieces, TENSOR, 0, 0, tiled=True)
    return jnp.sum(got.astype(jnp.float32), axis=0)


def gather_rows(rows):
    rows = lax.all_gather(rows, "tz", axis=0, tiled=True)
    return lax.all_gather(rows, ("ty", "tx"), axis=0, tiled=True)


def row_norm(inputs, gain):
    inputs = inputs.astype(jnp.float32)
    scale = lax.rsqrt(jnp.mean(inputs * inputs, axis=-1, keepdims=True) + epsilon)
    return inputs * scale * gain.astype(jnp.float32)


def rotate(inputs, position):
    half_dim = inputs.shape[-1] // 2
    frequency = rope_base ** (-2.0 * jnp.arange(half_dim, dtype=jnp.float32) / inputs.shape[-1])
    angles = position.astype(jnp.float32)[:, None] * frequency[None, :]
    cosine = jnp.cos(angles)[:, None, :]
    sine_part = jnp.sin(angles)[:, None, :]
    front = inputs[..., :half_dim]
    second = inputs[..., half_dim:]
    return jnp.concatenate(
        [front * cosine - second * sine_part, second * cosine + front * sine_part], axis=-1
    )


def prompt_layout(lengths_row, token_count):
    prompt_ends = jnp.cumsum(lengths_row)
    prompt_starts = prompt_ends - lengths_row
    row_ids = jnp.arange(token_count, dtype=jnp.int32)
    prompt = jnp.sum((row_ids[:, None] >= prompt_ends[None, :]).astype(jnp.int32), axis=1)
    inside = (row_ids[:, None] >= prompt_starts[None, :]) & (
        row_ids[:, None] < prompt_ends[None, :]
    )
    offset = jnp.sum(jnp.where(inside, prompt_starts[None, :], 0), axis=1)
    return (prompt, row_ids - offset, prompt_starts, prompt_ends)


def per_device(
    stream,
    lengths,
    page_table,
    request_prompt,
    attn_gain,
    query_gain,
    key_gain,
    mlp_gain,
    w_query,
    key_value_weight,
    w_out,
    w_gate,
    w_up,
    w_down,
):
    tok_dev = stream.shape[0]
    tensor_element_count = lax.axis_size(TENSOR)
    token_count = tok_dev * tensor_element_count
    my_index = lax.axis_index(TENSOR)
    heads_dev = w_query.shape[1] // HEAD_SIZE
    query_cols = heads_dev * HEAD_SIZE
    prompt, position, prompt_starts, prompt_ends = prompt_layout(lengths[0], token_count)
    portion = gather_rows(row_norm(stream, attn_gain).astype(jnp.bfloat16))
    joined = jnp.concatenate(
        [
            jnp.dot(portion, w_query, preferred_element_type=jnp.float32),
            jnp.dot(portion, key_value_weight, preferred_element_type=jnp.float32),
        ],
        axis=1,
    )
    queries = joined[:, :query_cols].reshape(token_count, heads_dev, HEAD_SIZE)
    kv_part = joined[:, query_cols:].astype(jnp.bfloat16)
    key_value_group = tensor_element_count // KEY_VALUE_HEADS
    for bit_id in range(key_value_group.bit_length() - 1):
        partner = partner_2(kv_part, TENSOR, bit_id)
        upper_half = my_index // 2**bit_id % 2
        kv_part = jnp.where(
            upper_half == 1,
            jnp.concatenate([partner, kv_part], axis=1),
            jnp.concatenate([kv_part, partner], axis=1),
        )
    key_flat = rotate(row_norm(kv_part[:, None, :HEAD_SIZE], key_gain), position).astype(
        jnp.bfloat16
    )[:, 0, :]
    value_matrix_rows = kv_part[:, HEAD_SIZE:]
    q_rot = rotate(row_norm(queries, query_gain), position).astype(jnp.bfloat16)
    piece_cols = key_value_weight.shape[1]
    head_rows = jnp.concatenate([key_flat, value_matrix_rows], axis=1)
    own_cols = lax.dynamic_slice_in_dim(
        head_rows, my_index % key_value_group * piece_cols, piece_cols, 1
    )
    page_count = token_count // PAGE_TOKENS
    page_rows = own_cols.reshape(page_count, PAGE_TOKENS, piece_cols)
    group_count = lax.axis_size("dp")
    capacity = page_count // group_count
    owners = page_table // page_count
    slot_ids = page_table % page_count
    hits = (owners[:, None] == jnp.arange(group_count, dtype=jnp.int32)[None, :]).astype(jnp.int32)
    order_in = jnp.sum((jnp.cumsum(hits, axis=0) - hits) * hits, axis=1)
    buffer_pos = owners * capacity + order_in
    source = (
        jnp.zeros((page_count,), jnp.int32)
        .at[buffer_pos]
        .set(jnp.arange(page_count, dtype=jnp.int32))
    )
    send_pages = page_rows[source].reshape(group_count, capacity, PAGE_TOKENS, piece_cols)
    send_slots = slot_ids[source].reshape(group_count, capacity)
    got_pages, got_slots = (
        lax.all_to_all(send_pages, "dp", split_axis=0, concat_axis=0, tiled=True),
        lax.all_to_all(send_slots, "dp", split_axis=0, concat_axis=0, tiled=True),
    )
    paged_key_value_cache = (
        jnp.zeros((page_count, PAGE_TOKENS, piece_cols), jnp.bfloat16)
        .at[got_slots.reshape(-1)]
        .set(got_pages.reshape(page_count, PAGE_TOKENS, piece_cols))
    )
    block_rows = min(512, token_count)
    block_total = token_count // block_rows
    score_scale = math.sqrt(HEAD_SIZE)
    all_ids = jnp.arange(token_count, dtype=jnp.int32)
    local_ids = jnp.arange(block_rows, dtype=jnp.int32)

    def dense_block(block_index):
        first_row = block_index * block_rows
        q_block = lax.dynamic_slice_in_dim(q_rot, first_row, block_rows, 0)
        q_prompt = lax.dynamic_slice_in_dim(prompt, first_row, block_rows, 0)
        row_ids = first_row + local_ids
        scores = (
            jnp.einsum("qhd,kd->hqk", q_block, key_flat, preferred_element_type=jnp.float32)
            / score_scale
        )
        allowed = ((q_prompt[:, None] == prompt[None, :]) & (row_ids[:, None] >= all_ids[None, :]))[
            None
        ]
        peak = jnp.max(jnp.where(allowed, scores, -jnp.inf), axis=2, keepdims=True)
        weight = jnp.where(allowed, jnp.exp(scores - peak), 0.0)
        total_weight = jnp.sum(weight, axis=2, keepdims=True)
        running = jnp.einsum(
            "hqk,kd->hqd",
            weight.astype(jnp.bfloat16),
            value_matrix_rows,
            preferred_element_type=jnp.float32,
        )
        return (running / total_weight).astype(jnp.bfloat16)

    block_ids = jnp.arange(block_total, dtype=jnp.int32)
    blocks_out = lax.map(dense_block, block_ids)
    attn = jnp.transpose(blocks_out, (0, 2, 1, 3)).reshape(token_count, query_cols)
    attn_sum = scatter_sum(
        jnp.dot(attn, w_out, preferred_element_type=jnp.float32).astype(jnp.bfloat16),
        tensor_element_count,
    )
    resid = (stream.astype(jnp.float32) + attn_sum).astype(jnp.bfloat16)
    portion = gather_rows(row_norm(resid, mlp_gain).astype(jnp.bfloat16))
    gate_rows = jnp.dot(portion, w_gate, preferred_element_type=jnp.float32)
    upward = jnp.dot(portion, w_up, preferred_element_type=jnp.float32)
    hidden = (jax.nn.silu(gate_rows) * upward).astype(jnp.bfloat16)
    mlp_sum = scatter_sum(
        jnp.dot(hidden, w_down, preferred_element_type=jnp.float32).astype(jnp.bfloat16),
        tensor_element_count,
    )
    layer_out = (resid.astype(jnp.float32) + mlp_sum).astype(jnp.bfloat16)
    my_rows = my_index * tok_dev + jnp.arange(tok_dev, dtype=jnp.int32)
    select = ((prompt_ends - 1)[:, None] == my_rows[None, :]).astype(jnp.bfloat16)
    end_terms = jnp.dot(select, layer_out, preferred_element_type=jnp.float32)
    end_blocks = end_terms.astype(jnp.bfloat16).reshape(
        end_terms.shape[0], tensor_element_count, -1
    )
    end_rows = scatter_sum(jnp.transpose(end_blocks, (1, 0, 2)), tensor_element_count)[0].astype(
        jnp.bfloat16
    )
    table = lax.all_gather(end_rows, "dp", axis=0, tiled=True)
    pick = (request_prompt[:, None] == jnp.arange(table.shape[0], dtype=jnp.int32)[None, :]).astype(
        jnp.bfloat16
    )
    request_state = jnp.dot(pick, table, preferred_element_type=jnp.float32).astype(jnp.bfloat16)
    return (layer_out, paged_key_value_cache, request_state)


def solution(mesh):
    placed = (
        P(("dp",) + TENSOR, None),
        P("dp", None),
        P("dp"),
        P("dp"),
        P(),
        P(),
        P(),
        P(),
        P(None, TENSOR),
        P(None, TENSOR),
        P(TENSOR, None),
        P(None, TENSOR),
        P(None, TENSOR),
        P(TENSOR, None),
    )
    dp_size = mesh.shape["dp"]
    fine = jax.sharding.Mesh(
        mesh.devices.reshape((dp_size,) + TENSOR_SHAPE), ("dp",) + TENSOR
    )
    return jax.shard_map(
        per_device,
        mesh=fine,
        in_specs=placed,
        out_specs=(P(("dp",) + TENSOR, None), P("dp", None, TENSOR), P("dp", TENSOR)),
        check_vma=False,
    )
```

```python
import math

import jax
import jax.numpy as jnp
from jax import lax
from jax.sharding import PartitionSpec as P

KEY_VALUE_HEADS = 8
HEAD_SIZE = 128
PAGE_TOKENS = 16
TENSOR = ("ty", "tx", "tz")
TENSOR_SHAPE = (4, 4, 2)


epsilon = 1e-06
rope_base = 1000000.0


def partner_2(value, axis, bit):
    mask = 2**bit
    pairs = [(source, source ^ mask) for source in range(lax.axis_size(axis))]
    return lax.ppermute(value, axis, pairs)


def scatter_sum(partial, parts):
    pieces = partial.reshape((parts, partial.shape[0] // parts) + partial.shape[1:])
    got = lax.all_to_all(pieces, TENSOR, 0, 0, tiled=True)
    return jnp.sum(got.astype(jnp.float32), axis=0)


def gather_rows(rows):
    rows = lax.all_gather(rows, "tz", axis=0, tiled=True)
    return lax.all_gather(rows, ("ty", "tx"), axis=0, tiled=True)


def row_norm(inputs, gain):
    inputs = inputs.astype(jnp.float32)
    scale = lax.rsqrt(jnp.mean(inputs * inputs, axis=-1, keepdims=True) + epsilon)
    return inputs * scale * gain.astype(jnp.float32)


def rotate(inputs, position):
    half_dim = inputs.shape[-1] // 2
    frequency = rope_base ** (-2.0 * jnp.arange(half_dim, dtype=jnp.float32) / inputs.shape[-1])
    angles = position.astype(jnp.float32)[:, None] * frequency[None, :]
    cosine = jnp.cos(angles)[:, None, :]
    sine_part = jnp.sin(angles)[:, None, :]
    front = inputs[..., :half_dim]
    second = inputs[..., half_dim:]
    return jnp.concatenate(
        [front * cosine - second * sine_part, second * cosine + front * sine_part], axis=-1
    )


def prompt_layout(lengths_row, token_count):
    prompt_ends = jnp.cumsum(lengths_row)
    prompt_starts = prompt_ends - lengths_row
    row_ids = jnp.arange(token_count, dtype=jnp.int32)
    prompt = jnp.sum((row_ids[:, None] >= prompt_ends[None, :]).astype(jnp.int32), axis=1)
    inside = (row_ids[:, None] >= prompt_starts[None, :]) & (
        row_ids[:, None] < prompt_ends[None, :]
    )
    offset = jnp.sum(jnp.where(inside, prompt_starts[None, :], 0), axis=1)
    return (prompt, row_ids - offset, prompt_starts, prompt_ends)


def per_device(
    stream,
    lengths,
    page_table,
    request_prompt,
    attn_gain,
    query_gain,
    key_gain,
    mlp_gain,
    w_query,
    key_value_weight,
    w_out,
    w_gate,
    w_up,
    w_down,
):
    tok_dev = stream.shape[0]
    tensor_element_count = lax.axis_size(TENSOR)
    token_count = tok_dev * tensor_element_count
    my_index = lax.axis_index(TENSOR)
    heads_dev = w_query.shape[1] // HEAD_SIZE
    query_cols = heads_dev * HEAD_SIZE
    prompt, position, prompt_starts, prompt_ends = prompt_layout(lengths[0], token_count)
    portion = gather_rows(row_norm(stream, attn_gain).astype(jnp.bfloat16))
    joined = jnp.concatenate(
        [
            jnp.dot(portion, w_query, preferred_element_type=jnp.float32),
            jnp.dot(portion, key_value_weight, preferred_element_type=jnp.float32),
        ],
        axis=1,
    )
    queries = joined[:, :query_cols].reshape(token_count, heads_dev, HEAD_SIZE)
    kv_part = joined[:, query_cols:].astype(jnp.bfloat16)
    key_value_group = tensor_element_count // KEY_VALUE_HEADS
    for bit_id in range(key_value_group.bit_length() - 1):
        partner = partner_2(kv_part, TENSOR, bit_id)
        upper_half = my_index // 2**bit_id % 2
        kv_part = jnp.where(
            upper_half == 1,
            jnp.concatenate([partner, kv_part], axis=1),
            jnp.concatenate([kv_part, partner], axis=1),
        )
    key_flat = rotate(row_norm(kv_part[:, None, :HEAD_SIZE], key_gain), position).astype(
        jnp.bfloat16
    )[:, 0, :]
    value_matrix_rows = kv_part[:, HEAD_SIZE:]
    q_rot = rotate(row_norm(queries, query_gain), position).astype(jnp.bfloat16)
    piece_cols = key_value_weight.shape[1]
    head_rows = jnp.concatenate([key_flat, value_matrix_rows], axis=1)
    own_cols = lax.dynamic_slice_in_dim(
        head_rows, my_index % key_value_group * piece_cols, piece_cols, 1
    )
    page_count = token_count // PAGE_TOKENS
    page_rows = own_cols.reshape(page_count, PAGE_TOKENS, piece_cols)
    group_count = lax.axis_size("dp")
    capacity = page_count // group_count
    owners = page_table // page_count
    slot_ids = page_table % page_count
    hits = (owners[:, None] == jnp.arange(group_count, dtype=jnp.int32)[None, :]).astype(jnp.int32)
    order_in = jnp.sum((jnp.cumsum(hits, axis=0) - hits) * hits, axis=1)
    buffer_pos = owners * capacity + order_in
    source = (
        jnp.zeros((page_count,), jnp.int32)
        .at[buffer_pos]
        .set(jnp.arange(page_count, dtype=jnp.int32))
    )
    send_pages = page_rows[source].reshape(group_count, capacity, PAGE_TOKENS, piece_cols)
    send_slots = slot_ids[source].reshape(group_count, capacity)
    got_pages, got_slots = (
        lax.all_to_all(send_pages, "dp", split_axis=0, concat_axis=0, tiled=True),
        lax.all_to_all(send_slots, "dp", split_axis=0, concat_axis=0, tiled=True),
    )
    paged_key_value_cache = (
        jnp.zeros((page_count, PAGE_TOKENS, piece_cols), jnp.bfloat16)
        .at[got_slots.reshape(-1)]
        .set(got_pages.reshape(page_count, PAGE_TOKENS, piece_cols))
    )
    block_rows = min(512, token_count)
    block_total = token_count // block_rows
    score_scale = math.sqrt(HEAD_SIZE)
    all_ids = jnp.arange(token_count, dtype=jnp.int32)
    local_ids = jnp.arange(block_rows, dtype=jnp.int32)

    def dense_block(block_index):
        first_row = block_index * block_rows
        q_block = lax.dynamic_slice_in_dim(q_rot, first_row, block_rows, 0)
        q_prompt = lax.dynamic_slice_in_dim(prompt, first_row, block_rows, 0)
        row_ids = first_row + local_ids
        scores = (
            jnp.einsum("qhd,kd->hqk", q_block, key_flat, preferred_element_type=jnp.float32)
            / score_scale
        )
        allowed = ((q_prompt[:, None] == prompt[None, :]) & (row_ids[:, None] >= all_ids[None, :]))[
            None
        ]
        peak = jnp.max(jnp.where(allowed, scores, -jnp.inf), axis=2, keepdims=True)
        weight = jnp.where(allowed, jnp.exp(scores - peak), 0.0)
        total_weight = jnp.sum(weight, axis=2, keepdims=True)
        running = jnp.einsum(
            "hqk,kd->hqd",
            weight.astype(jnp.bfloat16),
            value_matrix_rows,
            preferred_element_type=jnp.float32,
        )
        return (running / total_weight).astype(jnp.bfloat16)

    block_ids = jnp.arange(block_total, dtype=jnp.int32)
    blocks_out = lax.map(dense_block, block_ids)
    attn = jnp.transpose(blocks_out, (0, 2, 1, 3)).reshape(token_count, query_cols)
    paged_key_value_cache, attn = lax.optimization_barrier((paged_key_value_cache, attn))
    attn_sum = scatter_sum(
        jnp.dot(attn, w_out, preferred_element_type=jnp.float32).astype(jnp.bfloat16),
        tensor_element_count,
    )
    resid = (stream.astype(jnp.float32) + attn_sum).astype(jnp.bfloat16)
    portion = gather_rows(row_norm(resid, mlp_gain).astype(jnp.bfloat16))
    gate_rows = jnp.dot(portion, w_gate, preferred_element_type=jnp.float32)
    upward = jnp.dot(portion, w_up, preferred_element_type=jnp.float32)
    hidden = (jax.nn.silu(gate_rows) * upward).astype(jnp.bfloat16)
    mlp_sum = scatter_sum(
        jnp.dot(hidden, w_down, preferred_element_type=jnp.float32).astype(jnp.bfloat16),
        tensor_element_count,
    )
    layer_out = (resid.astype(jnp.float32) + mlp_sum).astype(jnp.bfloat16)
    my_rows = my_index * tok_dev + jnp.arange(tok_dev, dtype=jnp.int32)
    select = ((prompt_ends - 1)[:, None] == my_rows[None, :]).astype(jnp.bfloat16)
    end_terms = jnp.dot(select, layer_out, preferred_element_type=jnp.float32)
    end_blocks = end_terms.astype(jnp.bfloat16).reshape(
        end_terms.shape[0], tensor_element_count, -1
    )
    end_rows = scatter_sum(jnp.transpose(end_blocks, (1, 0, 2)), tensor_element_count)[0].astype(
        jnp.bfloat16
    )
    table = lax.all_gather(end_rows, "dp", axis=0, tiled=True)
    pick = (request_prompt[:, None] == jnp.arange(table.shape[0], dtype=jnp.int32)[None, :]).astype(
        jnp.bfloat16
    )
    request_state = jnp.dot(pick, table, preferred_element_type=jnp.float32).astype(jnp.bfloat16)
    return (layer_out, paged_key_value_cache, request_state)


def solution(mesh):
    placed = (
        P(("dp",) + TENSOR, None),
        P("dp", None),
        P("dp"),
        P("dp"),
        P(),
        P(),
        P(),
        P(),
        P(None, TENSOR),
        P(None, TENSOR),
        P(TENSOR, None),
        P(None, TENSOR),
        P(None, TENSOR),
        P(TENSOR, None),
    )
    dp_size = mesh.shape["dp"]
    fine = jax.sharding.Mesh(
        mesh.devices.reshape((dp_size,) + TENSOR_SHAPE), ("dp",) + TENSOR
    )
    return jax.shard_map(
        per_device,
        mesh=fine,
        in_specs=placed,
        out_specs=(P(("dp",) + TENSOR, None), P("dp", None, TENSOR), P("dp", TENSOR)),
        check_vma=False,
    )
```

```python
import math

import jax
import jax.numpy as jnp
from jax import lax
from jax.sharding import PartitionSpec as P

KEY_VALUE_HEADS = 8
HEAD_SIZE = 128
PAGE_TOKENS = 16
TENSOR = ("ty", "tx", "tz")
TENSOR_SHAPE = (4, 4, 2)


epsilon = 1e-06
rope_base = 1000000.0


def partner_2(value, axis, bit):
    mask = 2**bit
    pairs = [(source, source ^ mask) for source in range(lax.axis_size(axis))]
    return lax.ppermute(value, axis, pairs)


def scatter_sum(partial, parts):
    pieces = partial.reshape((parts, partial.shape[0] // parts) + partial.shape[1:])
    got = lax.all_to_all(pieces, TENSOR, 0, 0, tiled=True)
    return jnp.sum(got.astype(jnp.float32), axis=0)


def gather_rows(rows):
    rows = lax.all_gather(rows, "tz", axis=0, tiled=True)
    return lax.all_gather(rows, ("ty", "tx"), axis=0, tiled=True)


def row_norm(inputs, gain):
    inputs = inputs.astype(jnp.float32)
    scale = lax.rsqrt(jnp.mean(inputs * inputs, axis=-1, keepdims=True) + epsilon)
    return inputs * scale * gain.astype(jnp.float32)


def rotate(inputs, position):
    half_dim = inputs.shape[-1] // 2
    frequency = rope_base ** (-2.0 * jnp.arange(half_dim, dtype=jnp.float32) / inputs.shape[-1])
    angles = position.astype(jnp.float32)[:, None] * frequency[None, :]
    cosine = jnp.cos(angles)[:, None, :]
    sine_part = jnp.sin(angles)[:, None, :]
    front = inputs[..., :half_dim]
    second = inputs[..., half_dim:]
    return jnp.concatenate(
        [front * cosine - second * sine_part, second * cosine + front * sine_part], axis=-1
    )


def prompt_layout(lengths_row, token_count):
    prompt_ends = jnp.cumsum(lengths_row)
    prompt_starts = prompt_ends - lengths_row
    row_ids = jnp.arange(token_count, dtype=jnp.int32)
    prompt = jnp.sum((row_ids[:, None] >= prompt_ends[None, :]).astype(jnp.int32), axis=1)
    inside = (row_ids[:, None] >= prompt_starts[None, :]) & (
        row_ids[:, None] < prompt_ends[None, :]
    )
    offset = jnp.sum(jnp.where(inside, prompt_starts[None, :], 0), axis=1)
    return (prompt, row_ids - offset, prompt_starts, prompt_ends)


def per_device(
    stream,
    lengths,
    page_table,
    request_prompt,
    attn_gain,
    query_gain,
    key_gain,
    mlp_gain,
    w_query,
    key_value_weight,
    w_out,
    w_gate,
    w_up,
    w_down,
):
    tok_dev = stream.shape[0]
    tensor_element_count = lax.axis_size(TENSOR)
    token_count = tok_dev * tensor_element_count
    my_index = lax.axis_index(TENSOR)
    heads_dev = w_query.shape[1] // HEAD_SIZE
    query_cols = heads_dev * HEAD_SIZE
    prompt, position, prompt_starts, prompt_ends = prompt_layout(lengths[0], token_count)
    portion = gather_rows(row_norm(stream, attn_gain).astype(jnp.bfloat16))
    joined = jnp.concatenate(
        [
            jnp.dot(portion, w_query, preferred_element_type=jnp.float32),
            jnp.dot(portion, key_value_weight, preferred_element_type=jnp.float32),
        ],
        axis=1,
    )
    queries = joined[:, :query_cols].reshape(token_count, heads_dev, HEAD_SIZE)
    kv_part = joined[:, query_cols:].astype(jnp.bfloat16)
    key_value_group = tensor_element_count // KEY_VALUE_HEADS
    for bit_id in range(key_value_group.bit_length() - 1):
        partner = partner_2(kv_part, TENSOR, bit_id)
        upper_half = my_index // 2**bit_id % 2
        kv_part = jnp.where(
            upper_half == 1,
            jnp.concatenate([partner, kv_part], axis=1),
            jnp.concatenate([kv_part, partner], axis=1),
        )
    key_flat = rotate(row_norm(kv_part[:, None, :HEAD_SIZE], key_gain), position).astype(
        jnp.bfloat16
    )[:, 0, :]
    value_matrix_rows = kv_part[:, HEAD_SIZE:]
    q_rot = rotate(row_norm(queries, query_gain), position).astype(jnp.bfloat16)
    piece_cols = key_value_weight.shape[1]
    head_rows = jnp.concatenate([key_flat, value_matrix_rows], axis=1)
    own_cols = lax.dynamic_slice_in_dim(
        head_rows, my_index % key_value_group * piece_cols, piece_cols, 1
    )
    page_count = token_count // PAGE_TOKENS
    page_rows = own_cols.reshape(page_count, PAGE_TOKENS, piece_cols)
    group_count = lax.axis_size("dp")
    capacity = page_count // group_count
    owners = page_table // page_count
    slot_ids = page_table % page_count
    hits = (owners[:, None] == jnp.arange(group_count, dtype=jnp.int32)[None, :]).astype(jnp.int32)
    order_in = jnp.sum((jnp.cumsum(hits, axis=0) - hits) * hits, axis=1)
    buffer_pos = owners * capacity + order_in
    source = (
        jnp.zeros((page_count,), jnp.int32)
        .at[buffer_pos]
        .set(jnp.arange(page_count, dtype=jnp.int32))
    )
    send_pages = page_rows[source].reshape(group_count, capacity, PAGE_TOKENS, piece_cols)
    send_slots = slot_ids[source].reshape(group_count, capacity)
    got_pages, got_slots = (
        lax.all_to_all(send_pages, "dp", split_axis=0, concat_axis=0, tiled=True),
        lax.all_to_all(send_slots, "dp", split_axis=0, concat_axis=0, tiled=True),
    )
    paged_key_value_cache = (
        jnp.zeros((page_count, PAGE_TOKENS, piece_cols), jnp.bfloat16)
        .at[got_slots.reshape(-1)]
        .set(got_pages.reshape(page_count, PAGE_TOKENS, piece_cols))
    )
    block_rows = min(512, token_count)
    block_total = token_count // block_rows
    score_scale = math.sqrt(HEAD_SIZE)
    all_ids = jnp.arange(token_count, dtype=jnp.int32)
    local_ids = jnp.arange(block_rows, dtype=jnp.int32)

    def dense_block(block_index):
        first_row = block_index * block_rows
        q_block = lax.dynamic_slice_in_dim(q_rot, first_row, block_rows, 0)
        q_prompt = lax.dynamic_slice_in_dim(prompt, first_row, block_rows, 0)
        row_ids = first_row + local_ids
        scores = (
            jnp.einsum("qhd,kd->hqk", q_block, key_flat, preferred_element_type=jnp.float32)
            / score_scale
        )
        allowed = ((q_prompt[:, None] == prompt[None, :]) & (row_ids[:, None] >= all_ids[None, :]))[
            None
        ]
        peak = jnp.max(jnp.where(allowed, scores, -jnp.inf), axis=2, keepdims=True)
        weight = jnp.where(allowed, jnp.exp(scores - peak), 0.0)
        total_weight = jnp.sum(weight, axis=2, keepdims=True)
        running = jnp.einsum(
            "hqk,kd->hqd",
            weight.astype(jnp.bfloat16),
            value_matrix_rows,
            preferred_element_type=jnp.float32,
        )
        return (running / total_weight).astype(jnp.bfloat16)

    block_ids = jnp.arange(block_total, dtype=jnp.int32)
    blocks_out = lax.map(dense_block, block_ids)
    attn = jnp.transpose(blocks_out, (0, 2, 1, 3)).reshape(token_count, query_cols)
    attn_sum = scatter_sum(
        jnp.dot(attn, w_out, preferred_element_type=jnp.float32).astype(jnp.bfloat16),
        tensor_element_count,
    )
    resid = (stream.astype(jnp.float32) + attn_sum).astype(jnp.bfloat16)
    portion = gather_rows(row_norm(resid, mlp_gain).astype(jnp.bfloat16))
    gate_rows = jnp.dot(portion, w_gate, preferred_element_type=jnp.float32)
    upward = jnp.dot(portion, w_up, preferred_element_type=jnp.float32)
    hidden = (jax.nn.silu(gate_rows) * upward).astype(jnp.bfloat16)
    down = jnp.dot(hidden, w_down, preferred_element_type=jnp.float32).astype(jnp.bfloat16)
    width = down.shape[1]
    feat = width // tensor_element_count
    nprompt = prompt_ends.shape[0]
    end_pick = ((prompt_ends - 1)[:, None] == all_ids[None, :]).astype(jnp.bfloat16)
    end_hidden = jnp.dot(end_pick, hidden, preferred_element_type=jnp.float32).astype(jnp.bfloat16)
    end_down = jnp.dot(end_hidden, w_down, preferred_element_type=jnp.float32).astype(jnp.bfloat16)
    my_rows = my_index * tok_dev + jnp.arange(tok_dev, dtype=jnp.int32)
    select = ((prompt_ends - 1)[:, None] == my_rows[None, :]).astype(jnp.bfloat16)
    end_resid = jnp.dot(select, resid, preferred_element_type=jnp.float32).astype(jnp.bfloat16)

    def by_feature_block(rows):
        blocks = rows.reshape(nprompt, tensor_element_count, feat)
        return jnp.transpose(blocks, (1, 0, 2)).reshape(tensor_element_count, nprompt * feat)

    extra = jnp.concatenate([by_feature_block(end_down), by_feature_block(end_resid)], axis=1)
    extra_rows = -(-extra.shape[1] // width)
    extra = jnp.pad(extra, ((0, 0), (0, extra_rows * width - extra.shape[1])))
    payload = jnp.concatenate(
        [
            down.reshape(tensor_element_count, tok_dev, width),
            extra.reshape(tensor_element_count, extra_rows, width),
        ],
        axis=1,
    )
    got = lax.all_to_all(payload, TENSOR, 0, 0, tiled=True)
    summed = jnp.sum(got.astype(jnp.float32), axis=0)
    mlp_sum = summed[:tok_dev]
    layer_out = (resid.astype(jnp.float32) + mlp_sum).astype(jnp.bfloat16)
    tail = summed[tok_dev:].reshape(-1)
    end_rows = (
        (tail[: nprompt * feat] + tail[nprompt * feat : 2 * nprompt * feat])
        .reshape(nprompt, feat)
        .astype(jnp.bfloat16)
    )
    table = lax.all_gather(end_rows, "dp", axis=0, tiled=True)
    pick = (request_prompt[:, None] == jnp.arange(table.shape[0], dtype=jnp.int32)[None, :]).astype(
        jnp.bfloat16
    )
    request_state = jnp.dot(pick, table, preferred_element_type=jnp.float32).astype(jnp.bfloat16)
    return (layer_out, paged_key_value_cache, request_state)


def solution(mesh):
    placed = (
        P(("dp",) + TENSOR, None),
        P("dp", None),
        P("dp"),
        P("dp"),
        P(),
        P(),
        P(),
        P(),
        P(None, TENSOR),
        P(None, TENSOR),
        P(TENSOR, None),
        P(None, TENSOR),
        P(None, TENSOR),
        P(TENSOR, None),
    )
    dp_size = mesh.shape["dp"]
    fine = jax.sharding.Mesh(
        mesh.devices.reshape((dp_size,) + TENSOR_SHAPE), ("dp",) + TENSOR
    )
    return jax.shard_map(
        per_device,
        mesh=fine,
        in_specs=placed,
        out_specs=(P(("dp",) + TENSOR, None), P("dp", None, TENSOR), P("dp", TENSOR)),
        check_vma=False,
    )
```

```python
import math

import jax
import jax.numpy as jnp
from jax import lax
from jax.sharding import PartitionSpec as P

KEY_VALUE_HEADS = 8
HEAD_SIZE = 128
PAGE_TOKENS = 16
TENSOR = ("ty", "tx", "tz")
TENSOR_SHAPE = (4, 4, 2)


epsilon = 1e-06
rope_base = 1000000.0


def partner_2(value, axis, bit):
    mask = 2**bit
    pairs = [(source, source ^ mask) for source in range(lax.axis_size(axis))]
    return lax.ppermute(value, axis, pairs)


def scatter_sum(partial, parts):
    pieces = partial.reshape((parts, partial.shape[0] // parts) + partial.shape[1:])
    got = lax.all_to_all(pieces, TENSOR, 0, 0, tiled=True)
    return jnp.sum(got.astype(jnp.float32), axis=0)


def gather_rows(rows):
    rows = lax.all_gather(rows, "tz", axis=0, tiled=True)
    return lax.all_gather(rows, ("ty", "tx"), axis=0, tiled=True)


def row_norm(inputs, gain):
    inputs = inputs.astype(jnp.float32)
    scale = lax.rsqrt(jnp.mean(inputs * inputs, axis=-1, keepdims=True) + epsilon)
    return inputs * scale * gain.astype(jnp.float32)


def rotate(inputs, position):
    half_dim = inputs.shape[-1] // 2
    frequency = rope_base ** (-2.0 * jnp.arange(half_dim, dtype=jnp.float32) / inputs.shape[-1])
    angles = position.astype(jnp.float32)[:, None] * frequency[None, :]
    cosine = jnp.cos(angles)[:, None, :]
    sine_part = jnp.sin(angles)[:, None, :]
    front = inputs[..., :half_dim]
    second = inputs[..., half_dim:]
    return jnp.concatenate(
        [front * cosine - second * sine_part, second * cosine + front * sine_part], axis=-1
    )


def prompt_layout(lengths_row, token_count):
    prompt_ends = jnp.cumsum(lengths_row)
    prompt_starts = prompt_ends - lengths_row
    row_ids = jnp.arange(token_count, dtype=jnp.int32)
    prompt = jnp.sum((row_ids[:, None] >= prompt_ends[None, :]).astype(jnp.int32), axis=1)
    inside = (row_ids[:, None] >= prompt_starts[None, :]) & (
        row_ids[:, None] < prompt_ends[None, :]
    )
    offset = jnp.sum(jnp.where(inside, prompt_starts[None, :], 0), axis=1)
    return (prompt, row_ids - offset, prompt_starts, prompt_ends)


def per_device(
    stream,
    lengths,
    page_table,
    request_prompt,
    attn_gain,
    query_gain,
    key_gain,
    mlp_gain,
    w_query,
    key_value_weight,
    w_out,
    w_gate,
    w_up,
    w_down,
):
    tok_dev = stream.shape[0]
    tensor_element_count = lax.axis_size(TENSOR)
    token_count = tok_dev * tensor_element_count
    my_index = lax.axis_index(TENSOR)
    heads_dev = w_query.shape[1] // HEAD_SIZE
    query_cols = heads_dev * HEAD_SIZE
    prompt, position, prompt_starts, prompt_ends = prompt_layout(lengths[0], token_count)
    portion = gather_rows(row_norm(stream, attn_gain).astype(jnp.bfloat16))
    joined = jnp.concatenate(
        [
            jnp.dot(portion, w_query, preferred_element_type=jnp.float32),
            jnp.dot(portion, key_value_weight, preferred_element_type=jnp.float32),
        ],
        axis=1,
    )
    queries = joined[:, :query_cols].reshape(token_count, heads_dev, HEAD_SIZE)
    kv_part = joined[:, query_cols:].astype(jnp.bfloat16)
    key_value_group = tensor_element_count // KEY_VALUE_HEADS
    for bit_id in range(key_value_group.bit_length() - 1):
        partner = partner_2(kv_part, TENSOR, bit_id)
        upper_half = my_index // 2**bit_id % 2
        kv_part = jnp.where(
            upper_half == 1,
            jnp.concatenate([partner, kv_part], axis=1),
            jnp.concatenate([kv_part, partner], axis=1),
        )
    key_flat = rotate(row_norm(kv_part[:, None, :HEAD_SIZE], key_gain), position).astype(
        jnp.bfloat16
    )[:, 0, :]
    value_matrix_rows = kv_part[:, HEAD_SIZE:]
    q_rot = rotate(row_norm(queries, query_gain), position).astype(jnp.bfloat16)
    piece_cols = key_value_weight.shape[1]
    head_rows = jnp.concatenate([key_flat, value_matrix_rows], axis=1)
    own_cols = lax.dynamic_slice_in_dim(
        head_rows, my_index % key_value_group * piece_cols, piece_cols, 1
    )
    page_count = token_count // PAGE_TOKENS
    page_rows = own_cols.reshape(page_count, PAGE_TOKENS, piece_cols)
    group_count = lax.axis_size("dp")
    capacity = page_count // group_count
    owners = page_table // page_count
    slot_ids = page_table % page_count
    hits = (owners[:, None] == jnp.arange(group_count, dtype=jnp.int32)[None, :]).astype(jnp.int32)
    order_in = jnp.sum((jnp.cumsum(hits, axis=0) - hits) * hits, axis=1)
    buffer_pos = owners * capacity + order_in
    source = (
        jnp.zeros((page_count,), jnp.int32)
        .at[buffer_pos]
        .set(jnp.arange(page_count, dtype=jnp.int32))
    )
    send_pages = page_rows[source].reshape(group_count, capacity, PAGE_TOKENS, piece_cols)
    send_slots = slot_ids[source].reshape(group_count, capacity)
    got_pages, got_slots = (
        lax.all_to_all(send_pages, "dp", split_axis=0, concat_axis=0, tiled=True),
        lax.all_to_all(send_slots, "dp", split_axis=0, concat_axis=0, tiled=True),
    )
    paged_key_value_cache = (
        jnp.zeros((page_count, PAGE_TOKENS, piece_cols), jnp.bfloat16)
        .at[got_slots.reshape(-1)]
        .set(got_pages.reshape(page_count, PAGE_TOKENS, piece_cols))
    )
    block_rows = min(512, token_count)
    block_total = token_count // block_rows
    score_scale = math.sqrt(HEAD_SIZE)
    all_ids = jnp.arange(token_count, dtype=jnp.int32)
    local_ids = jnp.arange(block_rows, dtype=jnp.int32)

    def dense_block(block_index):
        first_row = block_index * block_rows
        q_block = lax.dynamic_slice_in_dim(q_rot, first_row, block_rows, 0)
        q_prompt = lax.dynamic_slice_in_dim(prompt, first_row, block_rows, 0)
        row_ids = first_row + local_ids
        scores = (
            jnp.einsum("qhd,kd->hqk", q_block, key_flat, preferred_element_type=jnp.float32)
            / score_scale
        )
        allowed = ((q_prompt[:, None] == prompt[None, :]) & (row_ids[:, None] >= all_ids[None, :]))[
            None
        ]
        peak = jnp.max(jnp.where(allowed, scores, -jnp.inf), axis=2, keepdims=True)
        weight = jnp.where(allowed, jnp.exp(scores - peak), 0.0)
        total_weight = jnp.sum(weight, axis=2, keepdims=True)
        running = jnp.einsum(
            "hqk,kd->hqd",
            weight.astype(jnp.bfloat16),
            value_matrix_rows,
            preferred_element_type=jnp.float32,
        )
        return (running / total_weight).astype(jnp.bfloat16)

    block_ids = jnp.arange(block_total, dtype=jnp.int32)
    blocks_out = lax.map(dense_block, block_ids)
    attn = jnp.transpose(blocks_out, (0, 2, 1, 3)).reshape(token_count, query_cols)
    attn_sum = scatter_sum(
        jnp.dot(attn, w_out, preferred_element_type=jnp.float32).astype(jnp.bfloat16),
        tensor_element_count,
    )
    resid = (stream.astype(jnp.float32) + attn_sum).astype(jnp.bfloat16)
    portion = gather_rows(row_norm(resid, mlp_gain).astype(jnp.bfloat16))
    paged_key_value_cache, portion = lax.optimization_barrier((paged_key_value_cache, portion))
    gate_rows = jnp.dot(portion, w_gate, preferred_element_type=jnp.float32)
    upward = jnp.dot(portion, w_up, preferred_element_type=jnp.float32)
    hidden = (jax.nn.silu(gate_rows) * upward).astype(jnp.bfloat16)
    down = jnp.dot(hidden, w_down, preferred_element_type=jnp.float32).astype(jnp.bfloat16)
    width = down.shape[1]
    feat = width // tensor_element_count
    nprompt = prompt_ends.shape[0]
    end_pick = ((prompt_ends - 1)[:, None] == all_ids[None, :]).astype(jnp.bfloat16)
    end_hidden = jnp.dot(end_pick, hidden, preferred_element_type=jnp.float32).astype(jnp.bfloat16)
    end_down = jnp.dot(end_hidden, w_down, preferred_element_type=jnp.float32).astype(jnp.bfloat16)
    my_rows = my_index * tok_dev + jnp.arange(tok_dev, dtype=jnp.int32)
    select = ((prompt_ends - 1)[:, None] == my_rows[None, :]).astype(jnp.bfloat16)
    end_resid = jnp.dot(select, resid, preferred_element_type=jnp.float32).astype(jnp.bfloat16)

    def by_feature_block(rows):
        blocks = rows.reshape(nprompt, tensor_element_count, feat)
        return jnp.transpose(blocks, (1, 0, 2)).reshape(tensor_element_count, nprompt * feat)

    extra = jnp.concatenate([by_feature_block(end_down), by_feature_block(end_resid)], axis=1)
    extra_rows = -(-extra.shape[1] // width)
    extra = jnp.pad(extra, ((0, 0), (0, extra_rows * width - extra.shape[1])))
    payload = jnp.concatenate(
        [
            down.reshape(tensor_element_count, tok_dev, width),
            extra.reshape(tensor_element_count, extra_rows, width),
        ],
        axis=1,
    )
    got = lax.all_to_all(payload, TENSOR, 0, 0, tiled=True)
    summed = jnp.sum(got.astype(jnp.float32), axis=0)
    mlp_sum = summed[:tok_dev]
    layer_out = (resid.astype(jnp.float32) + mlp_sum).astype(jnp.bfloat16)
    tail = summed[tok_dev:].reshape(-1)
    end_rows = (
        (tail[: nprompt * feat] + tail[nprompt * feat : 2 * nprompt * feat])
        .reshape(nprompt, feat)
        .astype(jnp.bfloat16)
    )
    table = lax.all_gather(end_rows, "dp", axis=0, tiled=True)
    pick = (request_prompt[:, None] == jnp.arange(table.shape[0], dtype=jnp.int32)[None, :]).astype(
        jnp.bfloat16
    )
    request_state = jnp.dot(pick, table, preferred_element_type=jnp.float32).astype(jnp.bfloat16)
    return (layer_out, paged_key_value_cache, request_state)


def solution(mesh):
    placed = (
        P(("dp",) + TENSOR, None),
        P("dp", None),
        P("dp"),
        P("dp"),
        P(),
        P(),
        P(),
        P(),
        P(None, TENSOR),
        P(None, TENSOR),
        P(TENSOR, None),
        P(None, TENSOR),
        P(None, TENSOR),
        P(TENSOR, None),
    )
    dp_size = mesh.shape["dp"]
    fine = jax.sharding.Mesh(
        mesh.devices.reshape((dp_size,) + TENSOR_SHAPE), ("dp",) + TENSOR
    )
    return jax.shard_map(
        per_device,
        mesh=fine,
        in_specs=placed,
        out_specs=(P(("dp",) + TENSOR, None), P("dp", None, TENSOR), P("dp", TENSOR)),
        check_vma=False,
    )
```

```python
import math

import jax
import jax.numpy as jnp
from jax import lax
from jax.sharding import PartitionSpec as P

KEY_VALUE_HEADS = 8
HEAD_SIZE = 128
PAGE_TOKENS = 16
TENSOR = ("ty", "tx", "tz")
TENSOR_SHAPE = (4, 4, 2)


epsilon = 1e-06
rope_base = 1000000.0


def partner_2(value, axis, bit):
    mask = 2**bit
    pairs = [(source, source ^ mask) for source in range(lax.axis_size(axis))]
    return lax.ppermute(value, axis, pairs)


def scatter_sum(partial, parts):
    pieces = partial.reshape((parts, partial.shape[0] // parts) + partial.shape[1:])
    got = lax.all_to_all(pieces, TENSOR, 0, 0, tiled=True)
    return jnp.sum(got.astype(jnp.float32), axis=0)


def gather_rows(rows):
    rows = lax.all_gather(rows, "tz", axis=0, tiled=True)
    return lax.all_gather(rows, ("ty", "tx"), axis=0, tiled=True)


def row_norm(inputs, gain):
    inputs = inputs.astype(jnp.float32)
    scale = lax.rsqrt(jnp.mean(inputs * inputs, axis=-1, keepdims=True) + epsilon)
    return inputs * scale * gain.astype(jnp.float32)


def rotate(inputs, position):
    half_dim = inputs.shape[-1] // 2
    frequency = rope_base ** (-2.0 * jnp.arange(half_dim, dtype=jnp.float32) / inputs.shape[-1])
    angles = position.astype(jnp.float32)[:, None] * frequency[None, :]
    cosine = jnp.cos(angles)[:, None, :]
    sine_part = jnp.sin(angles)[:, None, :]
    front = inputs[..., :half_dim]
    second = inputs[..., half_dim:]
    return jnp.concatenate(
        [front * cosine - second * sine_part, second * cosine + front * sine_part], axis=-1
    )


def prompt_layout(lengths_row, token_count):
    prompt_ends = jnp.cumsum(lengths_row)
    prompt_starts = prompt_ends - lengths_row
    row_ids = jnp.arange(token_count, dtype=jnp.int32)
    prompt = jnp.sum((row_ids[:, None] >= prompt_ends[None, :]).astype(jnp.int32), axis=1)
    inside = (row_ids[:, None] >= prompt_starts[None, :]) & (
        row_ids[:, None] < prompt_ends[None, :]
    )
    offset = jnp.sum(jnp.where(inside, prompt_starts[None, :], 0), axis=1)
    return (prompt, row_ids - offset, prompt_starts, prompt_ends)


def per_device(
    stream,
    lengths,
    page_table,
    request_prompt,
    attn_gain,
    query_gain,
    key_gain,
    mlp_gain,
    w_query,
    key_value_weight,
    w_out,
    w_gate,
    w_up,
    w_down,
):
    tok_dev = stream.shape[0]
    tensor_element_count = lax.axis_size(TENSOR)
    token_count = tok_dev * tensor_element_count
    my_index = lax.axis_index(TENSOR)
    heads_dev = w_query.shape[1] // HEAD_SIZE
    query_cols = heads_dev * HEAD_SIZE
    prompt, position, prompt_starts, prompt_ends = prompt_layout(lengths[0], token_count)
    portion = gather_rows(row_norm(stream, attn_gain).astype(jnp.bfloat16))
    joined = jnp.concatenate(
        [
            jnp.dot(portion, w_query, preferred_element_type=jnp.float32),
            jnp.dot(portion, key_value_weight, preferred_element_type=jnp.float32),
        ],
        axis=1,
    )
    queries = joined[:, :query_cols].reshape(token_count, heads_dev, HEAD_SIZE)
    kv_part = joined[:, query_cols:].astype(jnp.bfloat16)
    key_value_group = tensor_element_count // KEY_VALUE_HEADS
    for bit_id in range(key_value_group.bit_length() - 1):
        partner = partner_2(kv_part, TENSOR, bit_id)
        upper_half = my_index // 2**bit_id % 2
        kv_part = jnp.where(
            upper_half == 1,
            jnp.concatenate([partner, kv_part], axis=1),
            jnp.concatenate([kv_part, partner], axis=1),
        )
    key_flat = rotate(row_norm(kv_part[:, None, :HEAD_SIZE], key_gain), position).astype(
        jnp.bfloat16
    )[:, 0, :]
    value_matrix_rows = kv_part[:, HEAD_SIZE:]
    q_rot = rotate(row_norm(queries, query_gain), position).astype(jnp.bfloat16)
    piece_cols = key_value_weight.shape[1]
    head_rows = jnp.concatenate([key_flat, value_matrix_rows], axis=1)
    own_cols = lax.dynamic_slice_in_dim(
        head_rows, my_index % key_value_group * piece_cols, piece_cols, 1
    )
    page_count = token_count // PAGE_TOKENS
    page_rows = own_cols.reshape(page_count, PAGE_TOKENS, piece_cols)
    group_count = lax.axis_size("dp")
    capacity = page_count // group_count
    owners = page_table // page_count
    slot_ids = page_table % page_count
    hits = (owners[:, None] == jnp.arange(group_count, dtype=jnp.int32)[None, :]).astype(jnp.int32)
    order_in = jnp.sum((jnp.cumsum(hits, axis=0) - hits) * hits, axis=1)
    buffer_pos = owners * capacity + order_in
    source = (
        jnp.zeros((page_count,), jnp.int32)
        .at[buffer_pos]
        .set(jnp.arange(page_count, dtype=jnp.int32))
    )
    send_pages = page_rows[source].reshape(group_count, capacity, PAGE_TOKENS, piece_cols)
    send_slots = slot_ids[source].reshape(group_count, capacity)
    got_pages, got_slots = (
        lax.all_to_all(send_pages, "dp", split_axis=0, concat_axis=0, tiled=True),
        lax.all_to_all(send_slots, "dp", split_axis=0, concat_axis=0, tiled=True),
    )
    paged_key_value_cache = (
        jnp.zeros((page_count, PAGE_TOKENS, piece_cols), jnp.bfloat16)
        .at[got_slots.reshape(-1)]
        .set(got_pages.reshape(page_count, PAGE_TOKENS, piece_cols))
    )
    block_rows = min(512, token_count)
    block_total = token_count // block_rows
    score_scale = math.sqrt(HEAD_SIZE)
    all_ids = jnp.arange(token_count, dtype=jnp.int32)
    local_ids = jnp.arange(block_rows, dtype=jnp.int32)

    def dense_block(block_index):
        first_row = block_index * block_rows
        q_block = lax.dynamic_slice_in_dim(q_rot, first_row, block_rows, 0)
        q_prompt = lax.dynamic_slice_in_dim(prompt, first_row, block_rows, 0)
        row_ids = first_row + local_ids
        scores = (
            jnp.einsum("qhd,kd->hqk", q_block, key_flat, preferred_element_type=jnp.float32)
            / score_scale
        )
        allowed = ((q_prompt[:, None] == prompt[None, :]) & (row_ids[:, None] >= all_ids[None, :]))[
            None
        ]
        peak = jnp.max(jnp.where(allowed, scores, -jnp.inf), axis=2, keepdims=True)
        weight = jnp.where(allowed, jnp.exp(scores - peak), 0.0)
        total_weight = jnp.sum(weight, axis=2, keepdims=True)
        running = jnp.einsum(
            "hqk,kd->hqd",
            weight.astype(jnp.bfloat16),
            value_matrix_rows,
            preferred_element_type=jnp.float32,
        )
        return (running / total_weight).astype(jnp.bfloat16)

    block_ids = jnp.arange(block_total, dtype=jnp.int32)
    blocks_out = lax.map(dense_block, block_ids)
    attn = jnp.transpose(blocks_out, (0, 2, 1, 3)).reshape(token_count, query_cols)
    attn_sum = scatter_sum(
        jnp.dot(attn, w_out, preferred_element_type=jnp.float32).astype(jnp.bfloat16),
        tensor_element_count,
    )
    resid = (stream.astype(jnp.float32) + attn_sum).astype(jnp.bfloat16)
    portion = gather_rows(row_norm(resid, mlp_gain).astype(jnp.bfloat16))
    paged_key_value_cache, portion = lax.optimization_barrier((paged_key_value_cache, portion))
    gate_rows = jnp.dot(portion, w_gate, preferred_element_type=jnp.float32)
    upward = jnp.dot(portion, w_up, preferred_element_type=jnp.float32)
    hidden = (jax.nn.silu(gate_rows) * upward).astype(jnp.bfloat16)
    down = jnp.dot(hidden, w_down, preferred_element_type=jnp.float32).astype(jnp.bfloat16)
    width = down.shape[1]
    feat = width // tensor_element_count
    nprompt = prompt_ends.shape[0]
    end_pick = ((prompt_ends - 1)[:, None] == all_ids[None, :]).astype(jnp.bfloat16)
    end_hidden = jnp.dot(end_pick, hidden, preferred_element_type=jnp.float32).astype(jnp.bfloat16)
    end_down = jnp.dot(end_hidden, w_down, preferred_element_type=jnp.float32).astype(jnp.bfloat16)
    my_rows = my_index * tok_dev + jnp.arange(tok_dev, dtype=jnp.int32)
    select = ((prompt_ends - 1)[:, None] == my_rows[None, :]).astype(jnp.bfloat16)
    end_resid = jnp.dot(select, resid, preferred_element_type=jnp.float32).astype(jnp.bfloat16)

    def by_feature_block(rows):
        blocks = rows.reshape(nprompt, tensor_element_count, feat)
        return jnp.transpose(blocks, (1, 0, 2)).reshape(tensor_element_count, nprompt * feat)

    extra = jnp.concatenate([by_feature_block(end_down), by_feature_block(end_resid)], axis=1)
    extra_rows = -(-extra.shape[1] // width)
    extra = jnp.pad(extra, ((0, 0), (0, extra_rows * width - extra.shape[1])))
    payload = jnp.concatenate(
        [down.reshape(tensor_element_count, tok_dev * width), extra], axis=1
    )
    got = lax.all_to_all(payload, TENSOR, 0, 0, tiled=True)
    summed = jnp.sum(got.astype(jnp.float32), axis=0).reshape(tok_dev + extra_rows, width)
    mlp_sum = summed[:tok_dev]
    layer_out = (resid.astype(jnp.float32) + mlp_sum).astype(jnp.bfloat16)
    tail = summed[tok_dev:].reshape(-1)
    end_rows = (
        (tail[: nprompt * feat] + tail[nprompt * feat : 2 * nprompt * feat])
        .reshape(nprompt, feat)
        .astype(jnp.bfloat16)
    )
    table = lax.all_gather(end_rows, "dp", axis=0, tiled=True)
    pick = (request_prompt[:, None] == jnp.arange(table.shape[0], dtype=jnp.int32)[None, :]).astype(
        jnp.bfloat16
    )
    request_state = jnp.dot(pick, table, preferred_element_type=jnp.float32).astype(jnp.bfloat16)
    return (layer_out, paged_key_value_cache, request_state)


def solution(mesh):
    placed = (
        P(("dp",) + TENSOR, None),
        P("dp", None),
        P("dp"),
        P("dp"),
        P(),
        P(),
        P(),
        P(),
        P(None, TENSOR),
        P(None, TENSOR),
        P(TENSOR, None),
        P(None, TENSOR),
        P(None, TENSOR),
        P(TENSOR, None),
    )
    dp_size = mesh.shape["dp"]
    fine = jax.sharding.Mesh(
        mesh.devices.reshape((dp_size,) + TENSOR_SHAPE), ("dp",) + TENSOR
    )
    return jax.shard_map(
        per_device,
        mesh=fine,
        in_specs=placed,
        out_specs=(P(("dp",) + TENSOR, None), P("dp", None, TENSOR), P("dp", TENSOR)),
        check_vma=False,
    )
```

```python
import math

import jax
import jax.numpy as jnp
from jax import lax
from jax.sharding import PartitionSpec as P

KEY_VALUE_HEADS = 8
HEAD_SIZE = 128
PAGE_TOKENS = 16
TENSOR = ("ty", "tx", "tz")
TENSOR_SHAPE = (4, 4, 2)


epsilon = 1e-06
rope_base = 1000000.0


def partner_2(value, axis, bit):
    mask = 2**bit
    pairs = [(source, source ^ mask) for source in range(lax.axis_size(axis))]
    return lax.ppermute(value, axis, pairs)


def scatter_sum(partial, parts):
    pieces = partial.reshape((parts, partial.shape[0] // parts) + partial.shape[1:])
    got = lax.all_to_all(pieces, TENSOR, 0, 0, tiled=True)
    return jnp.sum(got.astype(jnp.float32), axis=0)


def gather_rows(rows):
    rows = lax.all_gather(rows, "tz", axis=0, tiled=True)
    return lax.all_gather(rows, ("ty", "tx"), axis=0, tiled=True)


def row_norm(inputs, gain):
    inputs = inputs.astype(jnp.float32)
    scale = lax.rsqrt(jnp.mean(inputs * inputs, axis=-1, keepdims=True) + epsilon)
    return inputs * scale * gain.astype(jnp.float32)


def rotate(inputs, position):
    half_dim = inputs.shape[-1] // 2
    frequency = rope_base ** (-2.0 * jnp.arange(half_dim, dtype=jnp.float32) / inputs.shape[-1])
    angles = position.astype(jnp.float32)[:, None] * frequency[None, :]
    cosine = jnp.cos(angles)[:, None, :]
    sine_part = jnp.sin(angles)[:, None, :]
    front = inputs[..., :half_dim]
    second = inputs[..., half_dim:]
    return jnp.concatenate(
        [front * cosine - second * sine_part, second * cosine + front * sine_part], axis=-1
    )


def prompt_layout(lengths_row, token_count):
    prompt_ends = jnp.cumsum(lengths_row)
    prompt_starts = prompt_ends - lengths_row
    row_ids = jnp.arange(token_count, dtype=jnp.int32)
    prompt = jnp.sum((row_ids[:, None] >= prompt_ends[None, :]).astype(jnp.int32), axis=1)
    inside = (row_ids[:, None] >= prompt_starts[None, :]) & (
        row_ids[:, None] < prompt_ends[None, :]
    )
    offset = jnp.sum(jnp.where(inside, prompt_starts[None, :], 0), axis=1)
    return (prompt, row_ids - offset, prompt_starts, prompt_ends)


def per_device(
    stream,
    lengths,
    page_table,
    request_prompt,
    attn_gain,
    query_gain,
    key_gain,
    mlp_gain,
    w_query,
    key_value_weight,
    w_out,
    w_gate,
    w_up,
    w_down,
):
    tok_dev = stream.shape[0]
    tensor_element_count = lax.axis_size(TENSOR)
    token_count = tok_dev * tensor_element_count
    my_index = lax.axis_index(TENSOR)
    heads_dev = w_query.shape[1] // HEAD_SIZE
    query_cols = heads_dev * HEAD_SIZE
    prompt, position, prompt_starts, prompt_ends = prompt_layout(lengths[0], token_count)
    portion = gather_rows(row_norm(stream, attn_gain).astype(jnp.bfloat16))
    joined = jnp.concatenate(
        [
            jnp.dot(portion, w_query, preferred_element_type=jnp.float32),
            jnp.dot(portion, key_value_weight, preferred_element_type=jnp.float32),
        ],
        axis=1,
    )
    queries = joined[:, :query_cols].reshape(token_count, heads_dev, HEAD_SIZE)
    kv_part = joined[:, query_cols:].astype(jnp.bfloat16)
    key_value_group = tensor_element_count // KEY_VALUE_HEADS
    for bit_id in range(key_value_group.bit_length() - 1):
        partner = partner_2(kv_part, TENSOR, bit_id)
        upper_half = my_index // 2**bit_id % 2
        kv_part = jnp.where(
            upper_half == 1,
            jnp.concatenate([partner, kv_part], axis=1),
            jnp.concatenate([kv_part, partner], axis=1),
        )
    key_flat = rotate(row_norm(kv_part[:, None, :HEAD_SIZE], key_gain), position).astype(
        jnp.bfloat16
    )[:, 0, :]
    value_matrix_rows = kv_part[:, HEAD_SIZE:]
    q_rot = rotate(row_norm(queries, query_gain), position).astype(jnp.bfloat16)
    piece_cols = key_value_weight.shape[1]
    head_rows = jnp.concatenate([key_flat, value_matrix_rows], axis=1)
    own_cols = lax.dynamic_slice_in_dim(
        head_rows, my_index % key_value_group * piece_cols, piece_cols, 1
    )
    page_count = token_count // PAGE_TOKENS
    page_rows = own_cols.reshape(page_count, PAGE_TOKENS, piece_cols)
    group_count = lax.axis_size("dp")
    capacity = page_count // group_count
    owners = page_table // page_count
    slot_ids = page_table % page_count
    hits = (owners[:, None] == jnp.arange(group_count, dtype=jnp.int32)[None, :]).astype(jnp.int32)
    order_in = jnp.sum((jnp.cumsum(hits, axis=0) - hits) * hits, axis=1)
    buffer_pos = owners * capacity + order_in
    source = (
        jnp.zeros((page_count,), jnp.int32)
        .at[buffer_pos]
        .set(jnp.arange(page_count, dtype=jnp.int32))
    )
    send_pages = page_rows[source].reshape(group_count, capacity, PAGE_TOKENS, piece_cols)
    send_slots = slot_ids[source].reshape(group_count, capacity)
    got_pages, got_slots = (
        lax.all_to_all(send_pages, "dp", split_axis=0, concat_axis=0, tiled=True),
        lax.all_to_all(send_slots, "dp", split_axis=0, concat_axis=0, tiled=True),
    )
    paged_key_value_cache = (
        jnp.zeros((page_count, PAGE_TOKENS, piece_cols), jnp.bfloat16)
        .at[got_slots.reshape(-1)]
        .set(got_pages.reshape(page_count, PAGE_TOKENS, piece_cols))
    )
    block_rows = min(512, token_count)
    block_total = token_count // block_rows
    score_scale = math.sqrt(HEAD_SIZE)
    all_ids = jnp.arange(token_count, dtype=jnp.int32)
    local_ids = jnp.arange(block_rows, dtype=jnp.int32)

    def dense_block(block_index):
        first_row = block_index * block_rows
        q_block = lax.dynamic_slice_in_dim(q_rot, first_row, block_rows, 0)
        q_prompt = lax.dynamic_slice_in_dim(prompt, first_row, block_rows, 0)
        row_ids = first_row + local_ids
        scores = (
            jnp.einsum("qhd,kd->hqk", q_block, key_flat, preferred_element_type=jnp.float32)
            / score_scale
        )
        allowed = ((q_prompt[:, None] == prompt[None, :]) & (row_ids[:, None] >= all_ids[None, :]))[
            None
        ]
        peak = jnp.max(jnp.where(allowed, scores, -jnp.inf), axis=2, keepdims=True)
        weight = jnp.where(allowed, jnp.exp(scores - peak), 0.0)
        total_weight = jnp.sum(weight, axis=2, keepdims=True)
        running = jnp.einsum(
            "hqk,kd->hqd",
            weight.astype(jnp.bfloat16),
            value_matrix_rows,
            preferred_element_type=jnp.float32,
        )
        return (running / total_weight).astype(jnp.bfloat16)

    block_ids = jnp.arange(block_total, dtype=jnp.int32)
    blocks_out = lax.map(dense_block, block_ids)
    attn = jnp.transpose(blocks_out, (0, 2, 1, 3)).reshape(token_count, query_cols)
    attn_sum = scatter_sum(
        jnp.dot(attn, w_out, preferred_element_type=jnp.float32).astype(jnp.bfloat16),
        tensor_element_count,
    )
    resid = (stream.astype(jnp.float32) + attn_sum).astype(jnp.bfloat16)
    portion = gather_rows(row_norm(resid, mlp_gain).astype(jnp.bfloat16))
    paged_key_value_cache, portion = lax.optimization_barrier((paged_key_value_cache, portion))
    gate_rows = jnp.dot(portion, w_gate, preferred_element_type=jnp.float32)
    upward = jnp.dot(portion, w_up, preferred_element_type=jnp.float32)
    hidden = (jax.nn.silu(gate_rows) * upward).astype(jnp.bfloat16)
    mlp_sum = scatter_sum(
        jnp.dot(hidden, w_down, preferred_element_type=jnp.float32).astype(jnp.bfloat16),
        tensor_element_count,
    )
    layer_out = (resid.astype(jnp.float32) + mlp_sum).astype(jnp.bfloat16)
    my_rows = my_index * tok_dev + jnp.arange(tok_dev, dtype=jnp.int32)
    select = ((prompt_ends - 1)[:, None] == my_rows[None, :]).astype(jnp.bfloat16)
    end_terms = jnp.dot(select, layer_out, preferred_element_type=jnp.float32)
    end_blocks = end_terms.astype(jnp.bfloat16).reshape(
        end_terms.shape[0], tensor_element_count, -1
    )
    end_rows = scatter_sum(jnp.transpose(end_blocks, (1, 0, 2)), tensor_element_count)[0].astype(
        jnp.bfloat16
    )
    table = lax.all_gather(end_rows, "dp", axis=0, tiled=True)
    pick = (request_prompt[:, None] == jnp.arange(table.shape[0], dtype=jnp.int32)[None, :]).astype(
        jnp.bfloat16
    )
    request_state = jnp.dot(pick, table, preferred_element_type=jnp.float32).astype(jnp.bfloat16)
    return (layer_out, paged_key_value_cache, request_state)


def solution(mesh):
    placed = (
        P(("dp",) + TENSOR, None),
        P("dp", None),
        P("dp"),
        P("dp"),
        P(),
        P(),
        P(),
        P(),
        P(None, TENSOR),
        P(None, TENSOR),
        P(TENSOR, None),
        P(None, TENSOR),
        P(None, TENSOR),
        P(TENSOR, None),
    )
    dp_size = mesh.shape["dp"]
    fine = jax.sharding.Mesh(
        mesh.devices.reshape((dp_size,) + TENSOR_SHAPE), ("dp",) + TENSOR
    )
    return jax.shard_map(
        per_device,
        mesh=fine,
        in_specs=placed,
        out_specs=(P(("dp",) + TENSOR, None), P("dp", None, TENSOR), P("dp", TENSOR)),
        check_vma=False,
    )
```

```python
import math

import jax
import jax.numpy as jnp
from jax import lax
from jax.sharding import PartitionSpec as P

KEY_VALUE_HEADS = 8
HEAD_SIZE = 128
PAGE_TOKENS = 16
TENSOR = ("ty", "tx", "tz")
TENSOR_SHAPE = (4, 4, 2)


epsilon = 1e-06
rope_base = 1000000.0


def partner_2(value, axis, bit):
    mask = 2**bit
    pairs = [(source, source ^ mask) for source in range(lax.axis_size(axis))]
    return lax.ppermute(value, axis, pairs)


def scatter_sum(partial, parts):
    pieces = partial.reshape((parts, partial.shape[0] // parts) + partial.shape[1:])
    got = lax.all_to_all(pieces, TENSOR, 0, 0, tiled=True)
    return jnp.sum(got.astype(jnp.float32), axis=0)


def gather_rows(rows):
    rows = lax.all_gather(rows, "tz", axis=0, tiled=True)
    return lax.all_gather(rows, ("ty", "tx"), axis=0, tiled=True)


def row_norm(inputs, gain):
    inputs = inputs.astype(jnp.float32)
    scale = lax.rsqrt(jnp.mean(inputs * inputs, axis=-1, keepdims=True) + epsilon)
    return inputs * scale * gain.astype(jnp.float32)


def rotate(inputs, position):
    half_dim = inputs.shape[-1] // 2
    frequency = rope_base ** (-2.0 * jnp.arange(half_dim, dtype=jnp.float32) / inputs.shape[-1])
    angles = position.astype(jnp.float32)[:, None] * frequency[None, :]
    cosine = jnp.cos(angles)[:, None, :]
    sine_part = jnp.sin(angles)[:, None, :]
    front = inputs[..., :half_dim]
    second = inputs[..., half_dim:]
    return jnp.concatenate(
        [front * cosine - second * sine_part, second * cosine + front * sine_part], axis=-1
    )


def prompt_layout(lengths_row, token_count):
    prompt_ends = jnp.cumsum(lengths_row)
    prompt_starts = prompt_ends - lengths_row
    row_ids = jnp.arange(token_count, dtype=jnp.int32)
    prompt = jnp.sum((row_ids[:, None] >= prompt_ends[None, :]).astype(jnp.int32), axis=1)
    inside = (row_ids[:, None] >= prompt_starts[None, :]) & (
        row_ids[:, None] < prompt_ends[None, :]
    )
    offset = jnp.sum(jnp.where(inside, prompt_starts[None, :], 0), axis=1)
    return (prompt, row_ids - offset, prompt_starts, prompt_ends)


def per_device(
    stream,
    lengths,
    page_table,
    request_prompt,
    attn_gain,
    query_gain,
    key_gain,
    mlp_gain,
    w_query,
    key_value_weight,
    w_out,
    w_gate,
    w_up,
    w_down,
):
    tok_dev = stream.shape[0]
    tensor_element_count = lax.axis_size(TENSOR)
    token_count = tok_dev * tensor_element_count
    my_index = lax.axis_index(TENSOR)
    heads_dev = w_query.shape[1] // HEAD_SIZE
    query_cols = heads_dev * HEAD_SIZE
    prompt, position, prompt_starts, prompt_ends = prompt_layout(lengths[0], token_count)
    portion = gather_rows(row_norm(stream, attn_gain).astype(jnp.bfloat16))
    key_value_group = tensor_element_count // KEY_VALUE_HEADS
    head_weight = key_value_weight
    for bit_id in range(key_value_group.bit_length() - 1):
        partner = partner_2(head_weight, TENSOR, bit_id)
        upper_half = my_index // 2**bit_id % 2
        head_weight = jnp.where(
            upper_half == 1,
            jnp.concatenate([partner, head_weight], axis=1),
            jnp.concatenate([head_weight, partner], axis=1),
        )
    joined = jnp.concatenate(
        [
            jnp.dot(portion, w_query, preferred_element_type=jnp.float32),
            jnp.dot(portion, head_weight, preferred_element_type=jnp.float32),
        ],
        axis=1,
    )
    queries = joined[:, :query_cols].reshape(token_count, heads_dev, HEAD_SIZE)
    kv_part = joined[:, query_cols:].astype(jnp.bfloat16)
    key_flat = rotate(row_norm(kv_part[:, None, :HEAD_SIZE], key_gain), position).astype(
        jnp.bfloat16
    )[:, 0, :]
    value_matrix_rows = kv_part[:, HEAD_SIZE:]
    q_rot = rotate(row_norm(queries, query_gain), position).astype(jnp.bfloat16)
    piece_cols = key_value_weight.shape[1]
    head_rows = jnp.concatenate([key_flat, value_matrix_rows], axis=1)
    own_cols = lax.dynamic_slice_in_dim(
        head_rows, my_index % key_value_group * piece_cols, piece_cols, 1
    )
    page_count = token_count // PAGE_TOKENS
    page_rows = own_cols.reshape(page_count, PAGE_TOKENS, piece_cols)
    group_count = lax.axis_size("dp")
    capacity = page_count // group_count
    owners = page_table // page_count
    slot_ids = page_table % page_count
    hits = (owners[:, None] == jnp.arange(group_count, dtype=jnp.int32)[None, :]).astype(jnp.int32)
    order_in = jnp.sum((jnp.cumsum(hits, axis=0) - hits) * hits, axis=1)
    buffer_pos = owners * capacity + order_in
    source = (
        jnp.zeros((page_count,), jnp.int32)
        .at[buffer_pos]
        .set(jnp.arange(page_count, dtype=jnp.int32))
    )
    send_pages = page_rows[source].reshape(group_count, capacity, PAGE_TOKENS, piece_cols)
    send_slots = slot_ids[source].reshape(group_count, capacity)
    got_pages, got_slots = (
        lax.all_to_all(send_pages, "dp", split_axis=0, concat_axis=0, tiled=True),
        lax.all_to_all(send_slots, "dp", split_axis=0, concat_axis=0, tiled=True),
    )
    paged_key_value_cache = (
        jnp.zeros((page_count, PAGE_TOKENS, piece_cols), jnp.bfloat16)
        .at[got_slots.reshape(-1)]
        .set(got_pages.reshape(page_count, PAGE_TOKENS, piece_cols))
    )
    block_rows = min(512, token_count)
    block_total = token_count // block_rows
    score_scale = math.sqrt(HEAD_SIZE)
    all_ids = jnp.arange(token_count, dtype=jnp.int32)
    local_ids = jnp.arange(block_rows, dtype=jnp.int32)

    def dense_block(block_index):
        first_row = block_index * block_rows
        q_block = lax.dynamic_slice_in_dim(q_rot, first_row, block_rows, 0)
        q_prompt = lax.dynamic_slice_in_dim(prompt, first_row, block_rows, 0)
        row_ids = first_row + local_ids
        scores = (
            jnp.einsum("qhd,kd->hqk", q_block, key_flat, preferred_element_type=jnp.float32)
            / score_scale
        )
        allowed = ((q_prompt[:, None] == prompt[None, :]) & (row_ids[:, None] >= all_ids[None, :]))[
            None
        ]
        peak = jnp.max(jnp.where(allowed, scores, -jnp.inf), axis=2, keepdims=True)
        weight = jnp.where(allowed, jnp.exp(scores - peak), 0.0)
        total_weight = jnp.sum(weight, axis=2, keepdims=True)
        running = jnp.einsum(
            "hqk,kd->hqd",
            weight.astype(jnp.bfloat16),
            value_matrix_rows,
            preferred_element_type=jnp.float32,
        )
        return (running / total_weight).astype(jnp.bfloat16)

    block_ids = jnp.arange(block_total, dtype=jnp.int32)
    blocks_out = lax.map(dense_block, block_ids)
    attn = jnp.transpose(blocks_out, (0, 2, 1, 3)).reshape(token_count, query_cols)
    attn_sum = scatter_sum(
        jnp.dot(attn, w_out, preferred_element_type=jnp.float32).astype(jnp.bfloat16),
        tensor_element_count,
    )
    resid = (stream.astype(jnp.float32) + attn_sum).astype(jnp.bfloat16)
    portion = gather_rows(row_norm(resid, mlp_gain).astype(jnp.bfloat16))
    paged_key_value_cache, portion = lax.optimization_barrier((paged_key_value_cache, portion))
    gate_rows = jnp.dot(portion, w_gate, preferred_element_type=jnp.float32)
    upward = jnp.dot(portion, w_up, preferred_element_type=jnp.float32)
    hidden = (jax.nn.silu(gate_rows) * upward).astype(jnp.bfloat16)
    mlp_sum = scatter_sum(
        jnp.dot(hidden, w_down, preferred_element_type=jnp.float32).astype(jnp.bfloat16),
        tensor_element_count,
    )
    layer_out = (resid.astype(jnp.float32) + mlp_sum).astype(jnp.bfloat16)
    my_rows = my_index * tok_dev + jnp.arange(tok_dev, dtype=jnp.int32)
    select = ((prompt_ends - 1)[:, None] == my_rows[None, :]).astype(jnp.bfloat16)
    end_terms = jnp.dot(select, layer_out, preferred_element_type=jnp.float32)
    end_blocks = end_terms.astype(jnp.bfloat16).reshape(
        end_terms.shape[0], tensor_element_count, -1
    )
    end_rows = scatter_sum(jnp.transpose(end_blocks, (1, 0, 2)), tensor_element_count)[0].astype(
        jnp.bfloat16
    )
    table = lax.all_gather(end_rows, "dp", axis=0, tiled=True)
    pick = (request_prompt[:, None] == jnp.arange(table.shape[0], dtype=jnp.int32)[None, :]).astype(
        jnp.bfloat16
    )
    request_state = jnp.dot(pick, table, preferred_element_type=jnp.float32).astype(jnp.bfloat16)
    return (layer_out, paged_key_value_cache, request_state)


def solution(mesh):
    placed = (
        P(("dp",) + TENSOR, None),
        P("dp", None),
        P("dp"),
        P("dp"),
        P(),
        P(),
        P(),
        P(),
        P(None, TENSOR),
        P(None, TENSOR),
        P(TENSOR, None),
        P(None, TENSOR),
        P(None, TENSOR),
        P(TENSOR, None),
    )
    dp_size = mesh.shape["dp"]
    fine = jax.sharding.Mesh(
        mesh.devices.reshape((dp_size,) + TENSOR_SHAPE), ("dp",) + TENSOR
    )
    return jax.shard_map(
        per_device,
        mesh=fine,
        in_specs=placed,
        out_specs=(P(("dp",) + TENSOR, None), P("dp", None, TENSOR), P("dp", TENSOR)),
        check_vma=False,
    )
```

```python
import math

import jax
import jax.numpy as jnp
from jax import lax
from jax.sharding import PartitionSpec as P

KEY_VALUE_HEADS = 8
HEAD_SIZE = 128
PAGE_TOKENS = 16
TENSOR = ("ty", "tx", "tz")
TENSOR_SHAPE = (4, 4, 2)


epsilon = 1e-06
rope_base = 1000000.0


def partner_2(value, axis, bit):
    mask = 2**bit
    pairs = [(source, source ^ mask) for source in range(lax.axis_size(axis))]
    return lax.ppermute(value, axis, pairs)


def scatter_sum(partial, parts):
    pieces = partial.reshape((parts, partial.shape[0] // parts) + partial.shape[1:])
    got = lax.all_to_all(pieces, TENSOR, 0, 0, tiled=True)
    return jnp.sum(got.astype(jnp.float32), axis=0)


def gather_rows(rows):
    rows = lax.all_gather(rows, "tz", axis=0, tiled=True)
    return lax.all_gather(rows, ("ty", "tx"), axis=0, tiled=True)


def row_norm(inputs, gain):
    inputs = inputs.astype(jnp.float32)
    scale = lax.rsqrt(jnp.mean(inputs * inputs, axis=-1, keepdims=True) + epsilon)
    return inputs * scale * gain.astype(jnp.float32)


def rotate(inputs, position):
    half_dim = inputs.shape[-1] // 2
    frequency = rope_base ** (-2.0 * jnp.arange(half_dim, dtype=jnp.float32) / inputs.shape[-1])
    angles = position.astype(jnp.float32)[:, None] * frequency[None, :]
    cosine = jnp.cos(angles)[:, None, :]
    sine_part = jnp.sin(angles)[:, None, :]
    front = inputs[..., :half_dim]
    second = inputs[..., half_dim:]
    return jnp.concatenate(
        [front * cosine - second * sine_part, second * cosine + front * sine_part], axis=-1
    )


def prompt_layout(lengths_row, token_count):
    prompt_ends = jnp.cumsum(lengths_row)
    prompt_starts = prompt_ends - lengths_row
    row_ids = jnp.arange(token_count, dtype=jnp.int32)
    prompt = jnp.sum((row_ids[:, None] >= prompt_ends[None, :]).astype(jnp.int32), axis=1)
    inside = (row_ids[:, None] >= prompt_starts[None, :]) & (
        row_ids[:, None] < prompt_ends[None, :]
    )
    offset = jnp.sum(jnp.where(inside, prompt_starts[None, :], 0), axis=1)
    return (prompt, row_ids - offset, prompt_starts, prompt_ends)


def per_device(
    stream,
    lengths,
    page_table,
    request_prompt,
    attn_gain,
    query_gain,
    key_gain,
    mlp_gain,
    w_query,
    key_value_weight,
    w_out,
    w_gate,
    w_up,
    w_down,
):
    tok_dev = stream.shape[0]
    tensor_element_count = lax.axis_size(TENSOR)
    token_count = tok_dev * tensor_element_count
    my_index = lax.axis_index(TENSOR)
    heads_dev = w_query.shape[1] // HEAD_SIZE
    query_cols = heads_dev * HEAD_SIZE
    prompt, position, prompt_starts, prompt_ends = prompt_layout(lengths[0], token_count)
    portion = gather_rows(row_norm(stream, attn_gain).astype(jnp.bfloat16))
    key_value_group = tensor_element_count // KEY_VALUE_HEADS
    head_weight = key_value_weight
    for bit_id in range(key_value_group.bit_length() - 1):
        partner = partner_2(head_weight, TENSOR, bit_id)
        upper_half = my_index // 2**bit_id % 2
        head_weight = jnp.where(
            upper_half == 1,
            jnp.concatenate([partner, head_weight], axis=1),
            jnp.concatenate([head_weight, partner], axis=1),
        )
    joined = jnp.concatenate(
        [
            jnp.dot(portion, w_query, preferred_element_type=jnp.float32),
            jnp.dot(portion, head_weight, preferred_element_type=jnp.float32),
        ],
        axis=1,
    )
    queries = joined[:, :query_cols].reshape(token_count, heads_dev, HEAD_SIZE)
    kv_part = joined[:, query_cols:].astype(jnp.bfloat16)
    key_flat = rotate(row_norm(kv_part[:, None, :HEAD_SIZE], key_gain), position).astype(
        jnp.bfloat16
    )[:, 0, :]
    value_matrix_rows = kv_part[:, HEAD_SIZE:]
    q_rot = rotate(row_norm(queries, query_gain), position).astype(jnp.bfloat16)
    piece_cols = key_value_weight.shape[1]
    head_rows = jnp.concatenate([key_flat, value_matrix_rows], axis=1)
    own_cols = lax.dynamic_slice_in_dim(
        head_rows, my_index % key_value_group * piece_cols, piece_cols, 1
    )
    page_count = token_count // PAGE_TOKENS
    page_rows = own_cols.reshape(page_count, PAGE_TOKENS, piece_cols)
    group_count = lax.axis_size("dp")
    capacity = page_count // group_count
    owners = page_table // page_count
    slot_ids = page_table % page_count
    hits = (owners[:, None] == jnp.arange(group_count, dtype=jnp.int32)[None, :]).astype(jnp.int32)
    order_in = jnp.sum((jnp.cumsum(hits, axis=0) - hits) * hits, axis=1)
    buffer_pos = owners * capacity + order_in
    source = (
        jnp.zeros((page_count,), jnp.int32)
        .at[buffer_pos]
        .set(jnp.arange(page_count, dtype=jnp.int32))
    )
    send_pages = page_rows[source].reshape(group_count, capacity, PAGE_TOKENS, piece_cols)
    send_slots = slot_ids[source].reshape(group_count, capacity)
    got_pages, got_slots = (
        lax.all_to_all(send_pages, "dp", split_axis=0, concat_axis=0, tiled=True),
        lax.all_to_all(send_slots, "dp", split_axis=0, concat_axis=0, tiled=True),
    )
    paged_key_value_cache = (
        jnp.zeros((page_count, PAGE_TOKENS, piece_cols), jnp.bfloat16)
        .at[got_slots.reshape(-1)]
        .set(got_pages.reshape(page_count, PAGE_TOKENS, piece_cols))
    )
    block_rows = min(512, token_count)
    block_total = token_count // block_rows
    score_scale = math.sqrt(HEAD_SIZE)
    all_ids = jnp.arange(token_count, dtype=jnp.int32)
    local_ids = jnp.arange(block_rows, dtype=jnp.int32)

    def dense_block(block_index):
        first_row = block_index * block_rows
        q_block = lax.dynamic_slice_in_dim(q_rot, first_row, block_rows, 0)
        q_prompt = lax.dynamic_slice_in_dim(prompt, first_row, block_rows, 0)
        row_ids = first_row + local_ids
        scores = (
            jnp.einsum("qhd,kd->hqk", q_block, key_flat, preferred_element_type=jnp.float32)
            / score_scale
        )
        allowed = ((q_prompt[:, None] == prompt[None, :]) & (row_ids[:, None] >= all_ids[None, :]))[
            None
        ]
        peak = jnp.max(jnp.where(allowed, scores, -jnp.inf), axis=2, keepdims=True)
        weight = jnp.where(allowed, jnp.exp(scores - peak), 0.0)
        total_weight = jnp.sum(weight, axis=2, keepdims=True)
        running = jnp.einsum(
            "hqk,kd->hqd",
            weight.astype(jnp.bfloat16),
            value_matrix_rows,
            preferred_element_type=jnp.float32,
        )
        return (running / total_weight).astype(jnp.bfloat16)

    block_ids = jnp.arange(block_total, dtype=jnp.int32)
    blocks_out = lax.map(dense_block, block_ids)
    attn = jnp.transpose(blocks_out, (0, 2, 1, 3)).reshape(token_count, query_cols)
    attn_sum = scatter_sum(
        jnp.dot(attn, w_out, preferred_element_type=jnp.float32).astype(jnp.bfloat16),
        tensor_element_count,
    )
    resid = (stream.astype(jnp.float32) + attn_sum).astype(jnp.bfloat16)
    portion = gather_rows(row_norm(resid, mlp_gain).astype(jnp.bfloat16))
    paged_key_value_cache, portion = lax.optimization_barrier((paged_key_value_cache, portion))
    gate_rows = jnp.dot(portion, w_gate, preferred_element_type=jnp.float32)
    upward = jnp.dot(portion, w_up, preferred_element_type=jnp.float32)
    hidden = (jax.nn.silu(gate_rows) * upward).astype(jnp.bfloat16)
    mlp_sum = scatter_sum(
        jnp.dot(hidden, w_down, preferred_element_type=jnp.float32).astype(jnp.bfloat16),
        tensor_element_count,
    )
    layer_out = (resid.astype(jnp.float32) + mlp_sum).astype(jnp.bfloat16)
    width = w_down.shape[1]
    feat = width // tensor_element_count
    nprompt = prompt_ends.shape[0]
    end_pick = ((prompt_ends - 1)[:, None] == all_ids[None, :]).astype(jnp.bfloat16)
    end_hidden = jnp.dot(end_pick, hidden, preferred_element_type=jnp.float32).astype(jnp.bfloat16)
    end_down = jnp.dot(end_hidden, w_down, preferred_element_type=jnp.float32).astype(jnp.bfloat16)
    my_rows = my_index * tok_dev + jnp.arange(tok_dev, dtype=jnp.int32)
    select = ((prompt_ends - 1)[:, None] == my_rows[None, :]).astype(jnp.bfloat16)
    end_resid = jnp.dot(select, resid, preferred_element_type=jnp.float32)
    end_terms = jnp.stack([end_down.astype(jnp.float32), end_resid])
    end_blocks = jnp.transpose(
        end_terms.reshape(2, nprompt, tensor_element_count, feat), (2, 0, 1, 3)
    )
    end_sums = lax.psum_scatter(end_blocks, TENSOR, scatter_dimension=0, tiled=True)[0]
    end_rows = (end_sums[0] + end_sums[1]).astype(jnp.bfloat16)
    table = lax.all_gather(end_rows, "dp", axis=0, tiled=True)
    pick = (request_prompt[:, None] == jnp.arange(table.shape[0], dtype=jnp.int32)[None, :]).astype(
        jnp.bfloat16
    )
    request_state = jnp.dot(pick, table, preferred_element_type=jnp.float32).astype(jnp.bfloat16)
    return (layer_out, paged_key_value_cache, request_state)


def solution(mesh):
    placed = (
        P(("dp",) + TENSOR, None),
        P("dp", None),
        P("dp"),
        P("dp"),
        P(),
        P(),
        P(),
        P(),
        P(None, TENSOR),
        P(None, TENSOR),
        P(TENSOR, None),
        P(None, TENSOR),
        P(None, TENSOR),
        P(TENSOR, None),
    )
    dp_size = mesh.shape["dp"]
    fine = jax.sharding.Mesh(
        mesh.devices.reshape((dp_size,) + TENSOR_SHAPE), ("dp",) + TENSOR
    )
    return jax.shard_map(
        per_device,
        mesh=fine,
        in_specs=placed,
        out_specs=(P(("dp",) + TENSOR, None), P("dp", None, TENSOR), P("dp", TENSOR)),
        check_vma=False,
    )
```

```python
import math

import jax
import jax.numpy as jnp
from jax import lax
from jax.sharding import PartitionSpec as P

KEY_VALUE_HEADS = 8
HEAD_SIZE = 128
PAGE_TOKENS = 16
TENSOR = ("ty", "tx", "tz")
TENSOR_SHAPE = (4, 4, 2)


epsilon = 1e-06
rope_base = 1000000.0


def partner_2(value, axis, bit):
    mask = 2**bit
    pairs = [(source, source ^ mask) for source in range(lax.axis_size(axis))]
    return lax.ppermute(value, axis, pairs)


def scatter_sum(partial, parts):
    pieces = partial.reshape((parts, partial.shape[0] // parts) + partial.shape[1:])
    got = lax.all_to_all(pieces, TENSOR, 0, 0, tiled=True)
    return jnp.sum(got.astype(jnp.float32), axis=0)


def gather_rows(rows):
    rows = lax.all_gather(rows, "tz", axis=0, tiled=True)
    return lax.all_gather(rows, ("ty", "tx"), axis=0, tiled=True)


def row_norm(inputs, gain):
    inputs = inputs.astype(jnp.float32)
    scale = lax.rsqrt(jnp.mean(inputs * inputs, axis=-1, keepdims=True) + epsilon)
    return inputs * scale * gain.astype(jnp.float32)


def rotate(inputs, position):
    half_dim = inputs.shape[-1] // 2
    frequency = rope_base ** (-2.0 * jnp.arange(half_dim, dtype=jnp.float32) / inputs.shape[-1])
    angles = position.astype(jnp.float32)[:, None] * frequency[None, :]
    cosine = jnp.cos(angles)[:, None, :]
    sine_part = jnp.sin(angles)[:, None, :]
    front = inputs[..., :half_dim]
    second = inputs[..., half_dim:]
    return jnp.concatenate(
        [front * cosine - second * sine_part, second * cosine + front * sine_part], axis=-1
    )


def prompt_layout(lengths_row, token_count):
    prompt_ends = jnp.cumsum(lengths_row)
    prompt_starts = prompt_ends - lengths_row
    row_ids = jnp.arange(token_count, dtype=jnp.int32)
    prompt = jnp.sum((row_ids[:, None] >= prompt_ends[None, :]).astype(jnp.int32), axis=1)
    inside = (row_ids[:, None] >= prompt_starts[None, :]) & (
        row_ids[:, None] < prompt_ends[None, :]
    )
    offset = jnp.sum(jnp.where(inside, prompt_starts[None, :], 0), axis=1)
    return (prompt, row_ids - offset, prompt_starts, prompt_ends)


def per_device(
    stream,
    lengths,
    page_table,
    request_prompt,
    attn_gain,
    query_gain,
    key_gain,
    mlp_gain,
    w_query,
    key_value_weight,
    w_out,
    w_gate,
    w_up,
    w_down,
):
    tok_dev = stream.shape[0]
    tensor_element_count = lax.axis_size(TENSOR)
    token_count = tok_dev * tensor_element_count
    my_index = lax.axis_index(TENSOR)
    heads_dev = w_query.shape[1] // HEAD_SIZE
    query_cols = heads_dev * HEAD_SIZE
    prompt, position, prompt_starts, prompt_ends = prompt_layout(lengths[0], token_count)
    portion = gather_rows(row_norm(stream, attn_gain).astype(jnp.bfloat16))
    key_value_group = tensor_element_count // KEY_VALUE_HEADS
    head_weight = key_value_weight
    for bit_id in range(key_value_group.bit_length() - 1):
        partner = partner_2(head_weight, TENSOR, bit_id)
        upper_half = my_index // 2**bit_id % 2
        head_weight = jnp.where(
            upper_half == 1,
            jnp.concatenate([partner, head_weight], axis=1),
            jnp.concatenate([head_weight, partner], axis=1),
        )
    joined = jnp.concatenate(
        [
            jnp.dot(portion, w_query, preferred_element_type=jnp.float32),
            jnp.dot(portion, head_weight, preferred_element_type=jnp.float32),
        ],
        axis=1,
    )
    queries = joined[:, :query_cols].reshape(token_count, heads_dev, HEAD_SIZE)
    kv_part = joined[:, query_cols:].astype(jnp.bfloat16)
    key_flat = rotate(row_norm(kv_part[:, None, :HEAD_SIZE], key_gain), position).astype(
        jnp.bfloat16
    )[:, 0, :]
    value_matrix_rows = kv_part[:, HEAD_SIZE:]
    q_rot = rotate(row_norm(queries, query_gain), position).astype(jnp.bfloat16)
    piece_cols = key_value_weight.shape[1]
    head_rows = jnp.concatenate([key_flat, value_matrix_rows], axis=1)
    own_cols = lax.dynamic_slice_in_dim(
        head_rows, my_index % key_value_group * piece_cols, piece_cols, 1
    )
    page_count = token_count // PAGE_TOKENS
    page_rows = own_cols.reshape(page_count, PAGE_TOKENS, piece_cols)
    group_count = lax.axis_size("dp")
    capacity = page_count // group_count
    owners = page_table // page_count
    slot_ids = page_table % page_count
    hits = (owners[:, None] == jnp.arange(group_count, dtype=jnp.int32)[None, :]).astype(jnp.int32)
    order_in = jnp.sum((jnp.cumsum(hits, axis=0) - hits) * hits, axis=1)
    buffer_pos = owners * capacity + order_in
    source = (
        jnp.zeros((page_count,), jnp.int32)
        .at[buffer_pos]
        .set(jnp.arange(page_count, dtype=jnp.int32))
    )
    send_pages = page_rows[source].reshape(group_count, capacity, PAGE_TOKENS, piece_cols)
    send_slots = slot_ids[source].reshape(group_count, capacity)
    got_pages, got_slots = (
        lax.all_to_all(send_pages, "dp", split_axis=0, concat_axis=0, tiled=True),
        lax.all_to_all(send_slots, "dp", split_axis=0, concat_axis=0, tiled=True),
    )
    paged_key_value_cache = (
        jnp.zeros((page_count, PAGE_TOKENS, piece_cols), jnp.bfloat16)
        .at[got_slots.reshape(-1)]
        .set(got_pages.reshape(page_count, PAGE_TOKENS, piece_cols))
    )
    block_rows = min(512, token_count)
    block_total = token_count // block_rows
    score_scale = math.sqrt(HEAD_SIZE)
    all_ids = jnp.arange(token_count, dtype=jnp.int32)
    local_ids = jnp.arange(block_rows, dtype=jnp.int32)

    def dense_block(block_index):
        first_row = block_index * block_rows
        key_count = first_row + block_rows
        q_block = q_rot[first_row:key_count]
        q_prompt = prompt[first_row:key_count]
        row_ids = first_row + local_ids
        scores = (
            jnp.einsum(
                "qhd,kd->hqk", q_block, key_flat[:key_count], preferred_element_type=jnp.float32
            )
            / score_scale
        )
        allowed = (
            (q_prompt[:, None] == prompt[None, :key_count])
            & (row_ids[:, None] >= all_ids[None, :key_count])
        )[None]
        peak = jnp.max(jnp.where(allowed, scores, -jnp.inf), axis=2, keepdims=True)
        weight = jnp.where(allowed, jnp.exp(scores - peak), 0.0)
        total_weight = jnp.sum(weight, axis=2, keepdims=True)
        running = jnp.einsum(
            "hqk,kd->hqd",
            weight.astype(jnp.bfloat16),
            value_matrix_rows[:key_count],
            preferred_element_type=jnp.float32,
        )
        return (running / total_weight).astype(jnp.bfloat16)

    blocks_out = jnp.stack([dense_block(block_index) for block_index in range(block_total)])
    attn = jnp.transpose(blocks_out, (0, 2, 1, 3)).reshape(token_count, query_cols)
    attn_sum = scatter_sum(
        jnp.dot(attn, w_out, preferred_element_type=jnp.float32).astype(jnp.bfloat16),
        tensor_element_count,
    )
    resid = (stream.astype(jnp.float32) + attn_sum).astype(jnp.bfloat16)
    portion = gather_rows(row_norm(resid, mlp_gain).astype(jnp.bfloat16))
    paged_key_value_cache, portion = lax.optimization_barrier((paged_key_value_cache, portion))
    gate_rows = jnp.dot(portion, w_gate, preferred_element_type=jnp.float32)
    upward = jnp.dot(portion, w_up, preferred_element_type=jnp.float32)
    hidden = (jax.nn.silu(gate_rows) * upward).astype(jnp.bfloat16)
    mlp_sum = scatter_sum(
        jnp.dot(hidden, w_down, preferred_element_type=jnp.float32).astype(jnp.bfloat16),
        tensor_element_count,
    )
    layer_out = (resid.astype(jnp.float32) + mlp_sum).astype(jnp.bfloat16)
    my_rows = my_index * tok_dev + jnp.arange(tok_dev, dtype=jnp.int32)
    select = ((prompt_ends - 1)[:, None] == my_rows[None, :]).astype(jnp.bfloat16)
    end_terms = jnp.dot(select, layer_out, preferred_element_type=jnp.float32)
    end_blocks = end_terms.astype(jnp.bfloat16).reshape(
        end_terms.shape[0], tensor_element_count, -1
    )
    end_rows = scatter_sum(jnp.transpose(end_blocks, (1, 0, 2)), tensor_element_count)[0].astype(
        jnp.bfloat16
    )
    table = lax.all_gather(end_rows, "dp", axis=0, tiled=True)
    pick = (request_prompt[:, None] == jnp.arange(table.shape[0], dtype=jnp.int32)[None, :]).astype(
        jnp.bfloat16
    )
    request_state = jnp.dot(pick, table, preferred_element_type=jnp.float32).astype(jnp.bfloat16)
    return (layer_out, paged_key_value_cache, request_state)


def solution(mesh):
    placed = (
        P(("dp",) + TENSOR, None),
        P("dp", None),
        P("dp"),
        P("dp"),
        P(),
        P(),
        P(),
        P(),
        P(None, TENSOR),
        P(None, TENSOR),
        P(TENSOR, None),
        P(None, TENSOR),
        P(None, TENSOR),
        P(TENSOR, None),
    )
    dp_size = mesh.shape["dp"]
    fine = jax.sharding.Mesh(
        mesh.devices.reshape((dp_size,) + TENSOR_SHAPE), ("dp",) + TENSOR
    )
    return jax.shard_map(
        per_device,
        mesh=fine,
        in_specs=placed,
        out_specs=(P(("dp",) + TENSOR, None), P("dp", None, TENSOR), P("dp", TENSOR)),
        check_vma=False,
    )
```

```python
import math

import jax
import jax.numpy as jnp
from jax import lax
from jax.sharding import PartitionSpec as P

KEY_VALUE_HEADS = 8
HEAD_SIZE = 128
PAGE_TOKENS = 16
TENSOR = ("ty", "tx", "tz")
TENSOR_SHAPE = (4, 4, 2)


epsilon = 1e-06
rope_base = 1000000.0


def partner_2(value, axis, bit):
    mask = 2**bit
    pairs = [(source, source ^ mask) for source in range(lax.axis_size(axis))]
    return lax.ppermute(value, axis, pairs)


def scatter_sum(partial, parts):
    pieces = partial.reshape((parts, partial.shape[0] // parts) + partial.shape[1:])
    got = lax.all_to_all(pieces, TENSOR, 0, 0, tiled=True)
    return jnp.sum(got.astype(jnp.float32), axis=0)


def gather_rows(rows):
    rows = lax.all_gather(rows, "tz", axis=0, tiled=True)
    return lax.all_gather(rows, ("ty", "tx"), axis=0, tiled=True)


def row_norm(inputs, gain):
    inputs = inputs.astype(jnp.float32)
    scale = lax.rsqrt(jnp.mean(inputs * inputs, axis=-1, keepdims=True) + epsilon)
    return inputs * scale * gain.astype(jnp.float32)


def rotate(inputs, position):
    half_dim = inputs.shape[-1] // 2
    frequency = rope_base ** (-2.0 * jnp.arange(half_dim, dtype=jnp.float32) / inputs.shape[-1])
    angles = position.astype(jnp.float32)[:, None] * frequency[None, :]
    cosine = jnp.cos(angles)[:, None, :]
    sine_part = jnp.sin(angles)[:, None, :]
    front = inputs[..., :half_dim]
    second = inputs[..., half_dim:]
    return jnp.concatenate(
        [front * cosine - second * sine_part, second * cosine + front * sine_part], axis=-1
    )


def prompt_layout(lengths_row, token_count):
    prompt_ends = jnp.cumsum(lengths_row)
    prompt_starts = prompt_ends - lengths_row
    row_ids = jnp.arange(token_count, dtype=jnp.int32)
    prompt = jnp.sum((row_ids[:, None] >= prompt_ends[None, :]).astype(jnp.int32), axis=1)
    inside = (row_ids[:, None] >= prompt_starts[None, :]) & (
        row_ids[:, None] < prompt_ends[None, :]
    )
    offset = jnp.sum(jnp.where(inside, prompt_starts[None, :], 0), axis=1)
    return (prompt, row_ids - offset, prompt_starts, prompt_ends)


def per_device(
    stream,
    lengths,
    page_table,
    request_prompt,
    attn_gain,
    query_gain,
    key_gain,
    mlp_gain,
    w_query,
    key_value_weight,
    w_out,
    w_gate,
    w_up,
    w_down,
):
    tok_dev = stream.shape[0]
    tensor_element_count = lax.axis_size(TENSOR)
    token_count = tok_dev * tensor_element_count
    my_index = lax.axis_index(TENSOR)
    heads_dev = w_query.shape[1] // HEAD_SIZE
    query_cols = heads_dev * HEAD_SIZE
    prompt, position, prompt_starts, prompt_ends = prompt_layout(lengths[0], token_count)
    portion = gather_rows(row_norm(stream, attn_gain).astype(jnp.bfloat16))
    key_value_group = tensor_element_count // KEY_VALUE_HEADS
    head_weight = key_value_weight
    for bit_id in range(key_value_group.bit_length() - 1):
        partner = partner_2(head_weight, TENSOR, bit_id)
        upper_half = my_index // 2**bit_id % 2
        head_weight = jnp.where(
            upper_half == 1,
            jnp.concatenate([partner, head_weight], axis=1),
            jnp.concatenate([head_weight, partner], axis=1),
        )
    joined = jnp.concatenate(
        [
            jnp.dot(portion, w_query, preferred_element_type=jnp.float32),
            jnp.dot(portion, head_weight, preferred_element_type=jnp.float32),
        ],
        axis=1,
    )
    queries = joined[:, :query_cols].reshape(token_count, heads_dev, HEAD_SIZE)
    kv_part = joined[:, query_cols:].astype(jnp.bfloat16)
    key_flat = rotate(row_norm(kv_part[:, None, :HEAD_SIZE], key_gain), position).astype(
        jnp.bfloat16
    )[:, 0, :]
    value_matrix_rows = kv_part[:, HEAD_SIZE:]
    q_rot = rotate(row_norm(queries, query_gain), position).astype(jnp.bfloat16)
    piece_cols = key_value_weight.shape[1]
    head_rows = jnp.concatenate([key_flat, value_matrix_rows], axis=1)
    own_cols = lax.dynamic_slice_in_dim(
        head_rows, my_index % key_value_group * piece_cols, piece_cols, 1
    )
    page_count = token_count // PAGE_TOKENS
    page_rows = own_cols.reshape(page_count, PAGE_TOKENS, piece_cols)
    group_count = lax.axis_size("dp")
    capacity = page_count // group_count
    owners = page_table // page_count
    slot_ids = page_table % page_count
    hits = (owners[:, None] == jnp.arange(group_count, dtype=jnp.int32)[None, :]).astype(jnp.int32)
    order_in = jnp.sum((jnp.cumsum(hits, axis=0) - hits) * hits, axis=1)
    buffer_pos = owners * capacity + order_in
    source = (
        jnp.zeros((page_count,), jnp.int32)
        .at[buffer_pos]
        .set(jnp.arange(page_count, dtype=jnp.int32))
    )
    send_pages = page_rows[source].reshape(group_count, capacity, PAGE_TOKENS, piece_cols)
    send_slots = slot_ids[source].reshape(group_count, capacity)
    got_pages, got_slots = (
        lax.all_to_all(send_pages, "dp", split_axis=0, concat_axis=0, tiled=True),
        lax.all_to_all(send_slots, "dp", split_axis=0, concat_axis=0, tiled=True),
    )
    paged_key_value_cache = (
        jnp.zeros((page_count, PAGE_TOKENS, piece_cols), jnp.bfloat16)
        .at[got_slots.reshape(-1)]
        .set(got_pages.reshape(page_count, PAGE_TOKENS, piece_cols))
    )
    block_rows = min(512, token_count)
    block_total = token_count // block_rows
    score_scale = math.sqrt(HEAD_SIZE)
    all_ids = jnp.arange(token_count, dtype=jnp.int32)
    local_ids = jnp.arange(block_rows, dtype=jnp.int32)

    def dense_block(block_index):
        first_row = block_index * block_rows
        key_count = first_row + block_rows
        q_block = q_rot[first_row:key_count]
        q_prompt = prompt[first_row:key_count]
        row_ids = first_row + local_ids
        scores = (
            jnp.einsum(
                "qhd,kd->hqk", q_block, key_flat[:key_count], preferred_element_type=jnp.float32
            )
            / score_scale
        )
        allowed = (
            (q_prompt[:, None] == prompt[None, :key_count])
            & (row_ids[:, None] >= all_ids[None, :key_count])
        )[None]
        peak = jnp.max(jnp.where(allowed, scores, -jnp.inf), axis=2, keepdims=True)
        weight = jnp.where(allowed, jnp.exp(scores - peak), 0.0)
        total_weight = jnp.sum(weight, axis=2, keepdims=True)
        running = jnp.einsum(
            "hqk,kd->hqd",
            weight.astype(jnp.bfloat16),
            value_matrix_rows[:key_count],
            preferred_element_type=jnp.float32,
        )
        return (running / total_weight).astype(jnp.bfloat16)

    blocks_out = jnp.stack([dense_block(block_index) for block_index in range(block_total)])
    attn = jnp.transpose(blocks_out, (0, 2, 1, 3)).reshape(token_count, query_cols)
    attn_sum = scatter_sum(
        jnp.dot(attn, w_out, preferred_element_type=jnp.float32).astype(jnp.bfloat16),
        tensor_element_count,
    )
    resid = (stream.astype(jnp.float32) + attn_sum).astype(jnp.bfloat16)
    portion = gather_rows(row_norm(resid, mlp_gain).astype(jnp.bfloat16))
    paged_key_value_cache, portion = lax.optimization_barrier((paged_key_value_cache, portion))
    gate_rows = jnp.dot(portion, w_gate, preferred_element_type=jnp.float32)
    upward = jnp.dot(portion, w_up, preferred_element_type=jnp.float32)
    hidden = (jax.nn.silu(gate_rows) * upward).astype(jnp.bfloat16)
    down = jnp.dot(hidden, w_down, preferred_element_type=jnp.float32).astype(jnp.bfloat16)
    width = down.shape[1]
    feat = width // tensor_element_count
    nprompt = prompt_ends.shape[0]
    end_pick = ((prompt_ends - 1)[:, None] == all_ids[None, :]).astype(jnp.bfloat16)
    end_hidden = jnp.dot(end_pick, hidden, preferred_element_type=jnp.float32).astype(jnp.bfloat16)
    end_down = jnp.dot(end_hidden, w_down, preferred_element_type=jnp.float32).astype(jnp.bfloat16)
    my_rows = my_index * tok_dev + jnp.arange(tok_dev, dtype=jnp.int32)
    select = ((prompt_ends - 1)[:, None] == my_rows[None, :]).astype(jnp.bfloat16)
    end_resid = jnp.dot(select, resid, preferred_element_type=jnp.float32).astype(jnp.bfloat16)

    def by_feature_block(rows):
        blocks = rows.reshape(nprompt, tensor_element_count, feat)
        return jnp.transpose(blocks, (1, 0, 2)).reshape(tensor_element_count, nprompt * feat)

    extra = jnp.concatenate([by_feature_block(end_down), by_feature_block(end_resid)], axis=1)
    extra_cols = 128
    extra = jnp.pad(extra, ((0, 0), (0, tok_dev * extra_cols - extra.shape[1])))
    payload = jnp.concatenate(
        [
            down.reshape(tensor_element_count, tok_dev, width),
            extra.reshape(tensor_element_count, tok_dev, extra_cols),
        ],
        axis=2,
    )
    got = lax.all_to_all(payload, TENSOR, 0, 0, tiled=True)
    summed = jnp.sum(got.astype(jnp.float32), axis=0)
    mlp_sum = summed[:, :width]
    layer_out = (resid.astype(jnp.float32) + mlp_sum).astype(jnp.bfloat16)
    tail = summed[:, width:].reshape(-1)
    end_rows = (
        (tail[: nprompt * feat] + tail[nprompt * feat : 2 * nprompt * feat])
        .reshape(nprompt, feat)
        .astype(jnp.bfloat16)
    )
    table = lax.all_gather(end_rows, "dp", axis=0, tiled=True)
    pick = (request_prompt[:, None] == jnp.arange(table.shape[0], dtype=jnp.int32)[None, :]).astype(
        jnp.bfloat16
    )
    request_state = jnp.dot(pick, table, preferred_element_type=jnp.float32).astype(jnp.bfloat16)
    return (layer_out, paged_key_value_cache, request_state)


def solution(mesh):
    placed = (
        P(("dp",) + TENSOR, None),
        P("dp", None),
        P("dp"),
        P("dp"),
        P(),
        P(),
        P(),
        P(),
        P(None, TENSOR),
        P(None, TENSOR),
        P(TENSOR, None),
        P(None, TENSOR),
        P(None, TENSOR),
        P(TENSOR, None),
    )
    dp_size = mesh.shape["dp"]
    fine = jax.sharding.Mesh(
        mesh.devices.reshape((dp_size,) + TENSOR_SHAPE), ("dp",) + TENSOR
    )
    return jax.shard_map(
        per_device,
        mesh=fine,
        in_specs=placed,
        out_specs=(P(("dp",) + TENSOR, None), P("dp", None, TENSOR), P("dp", TENSOR)),
        check_vma=False,
    )
```

```python
import math

import jax
import jax.numpy as jnp
from jax import lax
from jax.sharding import PartitionSpec as P

KEY_VALUE_HEADS = 8
HEAD_SIZE = 128
PAGE_TOKENS = 16
TENSOR = ("ty", "tx", "tz")
TENSOR_SHAPE = (4, 4, 2)


epsilon = 1e-06
rope_base = 1000000.0


def partner_2(value, axis, bit):
    mask = 2**bit
    pairs = [(source, source ^ mask) for source in range(lax.axis_size(axis))]
    return lax.ppermute(value, axis, pairs)


def scatter_sum(partial, parts):
    pieces = partial.reshape((parts, partial.shape[0] // parts) + partial.shape[1:])
    got = lax.all_to_all(pieces, TENSOR, 0, 0, tiled=True)
    return jnp.sum(got.astype(jnp.float32), axis=0)


def gather_rows(rows):
    rows = lax.all_gather(rows, "tz", axis=0, tiled=True)
    return lax.all_gather(rows, ("ty", "tx"), axis=0, tiled=True)


def row_norm(inputs, gain):
    inputs = inputs.astype(jnp.float32)
    scale = lax.rsqrt(jnp.mean(inputs * inputs, axis=-1, keepdims=True) + epsilon)
    return inputs * scale * gain.astype(jnp.float32)


def rotate(inputs, position):
    half_dim = inputs.shape[-1] // 2
    frequency = rope_base ** (-2.0 * jnp.arange(half_dim, dtype=jnp.float32) / inputs.shape[-1])
    angles = position.astype(jnp.float32)[:, None] * frequency[None, :]
    cosine = jnp.cos(angles)[:, None, :]
    sine_part = jnp.sin(angles)[:, None, :]
    front = inputs[..., :half_dim]
    second = inputs[..., half_dim:]
    return jnp.concatenate(
        [front * cosine - second * sine_part, second * cosine + front * sine_part], axis=-1
    )


def prompt_layout(lengths_row, token_count):
    prompt_ends = jnp.cumsum(lengths_row)
    prompt_starts = prompt_ends - lengths_row
    row_ids = jnp.arange(token_count, dtype=jnp.int32)
    prompt = jnp.sum((row_ids[:, None] >= prompt_ends[None, :]).astype(jnp.int32), axis=1)
    inside = (row_ids[:, None] >= prompt_starts[None, :]) & (
        row_ids[:, None] < prompt_ends[None, :]
    )
    offset = jnp.sum(jnp.where(inside, prompt_starts[None, :], 0), axis=1)
    return (prompt, row_ids - offset, prompt_starts, prompt_ends)


def per_device(
    stream,
    lengths,
    page_table,
    request_prompt,
    attn_gain,
    query_gain,
    key_gain,
    mlp_gain,
    w_query,
    key_value_weight,
    w_out,
    w_gate,
    w_up,
    w_down,
):
    tok_dev = stream.shape[0]
    tensor_element_count = lax.axis_size(TENSOR)
    token_count = tok_dev * tensor_element_count
    my_index = lax.axis_index(TENSOR)
    heads_dev = w_query.shape[1] // HEAD_SIZE
    query_cols = heads_dev * HEAD_SIZE
    prompt, position, prompt_starts, prompt_ends = prompt_layout(lengths[0], token_count)
    portion = gather_rows(row_norm(stream, attn_gain).astype(jnp.bfloat16))
    key_value_group = tensor_element_count // KEY_VALUE_HEADS
    head_weight = key_value_weight
    for bit_id in range(key_value_group.bit_length() - 1):
        partner = partner_2(head_weight, TENSOR, bit_id)
        upper_half = my_index // 2**bit_id % 2
        head_weight = jnp.where(
            upper_half == 1,
            jnp.concatenate([partner, head_weight], axis=1),
            jnp.concatenate([head_weight, partner], axis=1),
        )
    joined = jnp.concatenate(
        [
            jnp.dot(portion, w_query, preferred_element_type=jnp.float32),
            jnp.dot(portion, head_weight, preferred_element_type=jnp.float32),
        ],
        axis=1,
    )
    queries = joined[:, :query_cols].reshape(token_count, heads_dev, HEAD_SIZE)
    kv_part = joined[:, query_cols:].astype(jnp.bfloat16)
    key_flat = rotate(row_norm(kv_part[:, None, :HEAD_SIZE], key_gain), position).astype(
        jnp.bfloat16
    )[:, 0, :]
    value_matrix_rows = kv_part[:, HEAD_SIZE:]
    q_rot = rotate(row_norm(queries, query_gain), position).astype(jnp.bfloat16)
    piece_cols = key_value_weight.shape[1]
    head_rows = jnp.concatenate([key_flat, value_matrix_rows], axis=1)
    own_cols = lax.dynamic_slice_in_dim(
        head_rows, my_index % key_value_group * piece_cols, piece_cols, 1
    )
    page_count = token_count // PAGE_TOKENS
    page_rows = own_cols.reshape(page_count, PAGE_TOKENS, piece_cols)
    group_count = lax.axis_size("dp")
    capacity = page_count // group_count
    owners = page_table // page_count
    slot_ids = page_table % page_count
    hits = (owners[:, None] == jnp.arange(group_count, dtype=jnp.int32)[None, :]).astype(jnp.int32)
    order_in = jnp.sum((jnp.cumsum(hits, axis=0) - hits) * hits, axis=1)
    buffer_pos = owners * capacity + order_in
    source = (
        jnp.zeros((page_count,), jnp.int32)
        .at[buffer_pos]
        .set(jnp.arange(page_count, dtype=jnp.int32))
    )
    send_pages = page_rows[source].reshape(group_count, capacity, PAGE_TOKENS, piece_cols)
    send_slots = slot_ids[source].reshape(group_count, capacity)
    got_pages, got_slots = (
        lax.all_to_all(send_pages, "dp", split_axis=0, concat_axis=0, tiled=True),
        lax.all_to_all(send_slots, "dp", split_axis=0, concat_axis=0, tiled=True),
    )
    paged_key_value_cache = (
        jnp.zeros((page_count, PAGE_TOKENS, piece_cols), jnp.bfloat16)
        .at[got_slots.reshape(-1)]
        .set(got_pages.reshape(page_count, PAGE_TOKENS, piece_cols))
    )
    block_rows = min(512, token_count)
    block_total = token_count // block_rows
    score_scale = math.sqrt(HEAD_SIZE)
    all_ids = jnp.arange(token_count, dtype=jnp.int32)
    local_ids = jnp.arange(block_rows, dtype=jnp.int32)

    def dense_block(block_index):
        first_row = block_index * block_rows
        key_count = first_row + block_rows
        q_block = q_rot[first_row:key_count]
        q_prompt = prompt[first_row:key_count]
        row_ids = first_row + local_ids
        scores = (
            jnp.einsum(
                "qhd,kd->hqk", q_block, key_flat[:key_count], preferred_element_type=jnp.float32
            )
            / score_scale
        )
        allowed = (
            (q_prompt[:, None] == prompt[None, :key_count])
            & (row_ids[:, None] >= all_ids[None, :key_count])
        )[None]
        peak = jnp.max(jnp.where(allowed, scores, -jnp.inf), axis=2, keepdims=True)
        weight = jnp.where(allowed, jnp.exp(scores - peak), 0.0)
        total_weight = jnp.sum(weight, axis=2, keepdims=True)
        running = jnp.einsum(
            "hqk,kd->hqd",
            weight.astype(jnp.bfloat16),
            value_matrix_rows[:key_count],
            preferred_element_type=jnp.float32,
        )
        return (running / total_weight).astype(jnp.bfloat16)

    blocks_out = jnp.stack([dense_block(block_index) for block_index in range(block_total)])
    attn = jnp.transpose(blocks_out, (0, 2, 1, 3)).reshape(token_count, query_cols)
    attn_sum = scatter_sum(
        jnp.dot(attn, w_out, preferred_element_type=jnp.float32).astype(jnp.bfloat16),
        tensor_element_count,
    )
    resid = (stream.astype(jnp.float32) + attn_sum).astype(jnp.bfloat16)
    portion = gather_rows(row_norm(resid, mlp_gain).astype(jnp.bfloat16))
    paged_key_value_cache, portion = lax.optimization_barrier((paged_key_value_cache, portion))
    gate_rows = jnp.dot(portion, w_gate, preferred_element_type=jnp.float32)
    upward = jnp.dot(portion, w_up, preferred_element_type=jnp.float32)
    hidden = (jax.nn.silu(gate_rows) * upward).astype(jnp.bfloat16)
    width = w_down.shape[1]
    feat = width // tensor_element_count
    nprompt = prompt_ends.shape[0]
    end_pick = ((prompt_ends - 1)[:, None] == all_ids[None, :]).astype(jnp.bfloat16)
    end_hidden = jnp.dot(end_pick, hidden, preferred_element_type=jnp.float32).astype(jnp.bfloat16)
    end_down = jnp.dot(end_hidden, w_down, preferred_element_type=jnp.float32).astype(jnp.bfloat16)
    my_rows = my_index * tok_dev + jnp.arange(tok_dev, dtype=jnp.int32)
    select = ((prompt_ends - 1)[:, None] == my_rows[None, :]).astype(jnp.bfloat16)
    end_resid = jnp.dot(select, resid, preferred_element_type=jnp.float32).astype(jnp.bfloat16)

    def by_feature_block(rows):
        blocks = rows.reshape(nprompt, tensor_element_count, feat)
        return jnp.transpose(blocks, (1, 0, 2)).reshape(tensor_element_count, nprompt * feat)

    extra = jnp.concatenate([by_feature_block(end_down), by_feature_block(end_resid)], axis=1)
    extra_cols = 128
    extra = jnp.pad(extra, ((0, 0), (0, tok_dev * extra_cols - extra.shape[1])))
    wide_weight = jnp.concatenate(
        [w_down, jnp.zeros((w_down.shape[0], extra_cols), w_down.dtype)], axis=1
    )
    down = jnp.dot(hidden, wide_weight, preferred_element_type=jnp.float32).astype(jnp.bfloat16)
    payload = lax.dynamic_update_slice(
        down.reshape(tensor_element_count, tok_dev, width + extra_cols),
        extra.reshape(tensor_element_count, tok_dev, extra_cols),
        (0, 0, width),
    )
    got = lax.all_to_all(payload, TENSOR, 0, 0, tiled=True)
    summed = jnp.sum(got.astype(jnp.float32), axis=0)
    mlp_sum = summed[:, :width]
    layer_out = (resid.astype(jnp.float32) + mlp_sum).astype(jnp.bfloat16)
    tail = summed[:, width:].reshape(-1)
    end_rows = (
        (tail[: nprompt * feat] + tail[nprompt * feat : 2 * nprompt * feat])
        .reshape(nprompt, feat)
        .astype(jnp.bfloat16)
    )
    table = lax.all_gather(end_rows, "dp", axis=0, tiled=True)
    pick = (request_prompt[:, None] == jnp.arange(table.shape[0], dtype=jnp.int32)[None, :]).astype(
        jnp.bfloat16
    )
    request_state = jnp.dot(pick, table, preferred_element_type=jnp.float32).astype(jnp.bfloat16)
    return (layer_out, paged_key_value_cache, request_state)


def solution(mesh):
    placed = (
        P(("dp",) + TENSOR, None),
        P("dp", None),
        P("dp"),
        P("dp"),
        P(),
        P(),
        P(),
        P(),
        P(None, TENSOR),
        P(None, TENSOR),
        P(TENSOR, None),
        P(None, TENSOR),
        P(None, TENSOR),
        P(TENSOR, None),
    )
    dp_size = mesh.shape["dp"]
    fine = jax.sharding.Mesh(
        mesh.devices.reshape((dp_size,) + TENSOR_SHAPE), ("dp",) + TENSOR
    )
    return jax.shard_map(
        per_device,
        mesh=fine,
        in_specs=placed,
        out_specs=(P(("dp",) + TENSOR, None), P("dp", None, TENSOR), P("dp", TENSOR)),
        check_vma=False,
    )
```

```python
import math

import jax
import jax.numpy as jnp
from jax import lax
from jax.sharding import PartitionSpec as P

KEY_VALUE_HEADS = 8
HEAD_SIZE = 128
PAGE_TOKENS = 16
TENSOR = ("ty", "tx", "tz")
TENSOR_SHAPE = (4, 4, 2)


epsilon = 1e-06
rope_base = 1000000.0


def partner_2(value, axis, bit):
    mask = 2**bit
    pairs = [(source, source ^ mask) for source in range(lax.axis_size(axis))]
    return lax.ppermute(value, axis, pairs)


def scatter_sum(partial, parts):
    pieces = partial.reshape((parts, partial.shape[0] // parts) + partial.shape[1:])
    got = lax.all_to_all(pieces, TENSOR, 0, 0, tiled=True)
    return jnp.sum(got.astype(jnp.float32), axis=0)


def gather_rows(rows):
    partner = lax.ppermute(rows, "tz", [(0, 1), (1, 0)])
    rows = jnp.where(
        lax.axis_index("tz") == 0,
        jnp.concatenate([rows, partner], axis=0),
        jnp.concatenate([partner, rows], axis=0),
    )
    return lax.all_gather(rows, ("ty", "tx"), axis=0, tiled=True)


def row_norm(inputs, gain):
    inputs = inputs.astype(jnp.float32)
    scale = lax.rsqrt(jnp.mean(inputs * inputs, axis=-1, keepdims=True) + epsilon)
    return inputs * scale * gain.astype(jnp.float32)


def rotate(inputs, position):
    half_dim = inputs.shape[-1] // 2
    frequency = rope_base ** (-2.0 * jnp.arange(half_dim, dtype=jnp.float32) / inputs.shape[-1])
    angles = position.astype(jnp.float32)[:, None] * frequency[None, :]
    cosine = jnp.cos(angles)[:, None, :]
    sine_part = jnp.sin(angles)[:, None, :]
    front = inputs[..., :half_dim]
    second = inputs[..., half_dim:]
    return jnp.concatenate(
        [front * cosine - second * sine_part, second * cosine + front * sine_part], axis=-1
    )


def prompt_layout(lengths_row, token_count):
    prompt_ends = jnp.cumsum(lengths_row)
    prompt_starts = prompt_ends - lengths_row
    row_ids = jnp.arange(token_count, dtype=jnp.int32)
    prompt = jnp.sum((row_ids[:, None] >= prompt_ends[None, :]).astype(jnp.int32), axis=1)
    inside = (row_ids[:, None] >= prompt_starts[None, :]) & (
        row_ids[:, None] < prompt_ends[None, :]
    )
    offset = jnp.sum(jnp.where(inside, prompt_starts[None, :], 0), axis=1)
    return (prompt, row_ids - offset, prompt_starts, prompt_ends)


def per_device(
    stream,
    lengths,
    page_table,
    request_prompt,
    attn_gain,
    query_gain,
    key_gain,
    mlp_gain,
    w_query,
    key_value_weight,
    w_out,
    w_gate,
    w_up,
    w_down,
):
    tok_dev = stream.shape[0]
    tensor_element_count = lax.axis_size(TENSOR)
    token_count = tok_dev * tensor_element_count
    my_index = lax.axis_index(TENSOR)
    heads_dev = w_query.shape[1] // HEAD_SIZE
    query_cols = heads_dev * HEAD_SIZE
    prompt, position, prompt_starts, prompt_ends = prompt_layout(lengths[0], token_count)
    portion = gather_rows(row_norm(stream, attn_gain).astype(jnp.bfloat16))
    key_value_group = tensor_element_count // KEY_VALUE_HEADS
    head_weight = key_value_weight
    for bit_id in range(key_value_group.bit_length() - 1):
        partner = partner_2(head_weight, TENSOR, bit_id)
        upper_half = my_index // 2**bit_id % 2
        head_weight = jnp.where(
            upper_half == 1,
            jnp.concatenate([partner, head_weight], axis=1),
            jnp.concatenate([head_weight, partner], axis=1),
        )
    joined = jnp.concatenate(
        [
            jnp.dot(portion, w_query, preferred_element_type=jnp.float32),
            jnp.dot(portion, head_weight, preferred_element_type=jnp.float32),
        ],
        axis=1,
    )
    queries = joined[:, :query_cols].reshape(token_count, heads_dev, HEAD_SIZE)
    kv_part = joined[:, query_cols:].astype(jnp.bfloat16)
    key_flat = rotate(row_norm(kv_part[:, None, :HEAD_SIZE], key_gain), position).astype(
        jnp.bfloat16
    )[:, 0, :]
    value_matrix_rows = kv_part[:, HEAD_SIZE:]
    q_rot = rotate(row_norm(queries, query_gain), position).astype(jnp.bfloat16)
    piece_cols = key_value_weight.shape[1]
    head_rows = jnp.concatenate([key_flat, value_matrix_rows], axis=1)
    own_cols = lax.dynamic_slice_in_dim(
        head_rows, my_index % key_value_group * piece_cols, piece_cols, 1
    )
    page_count = token_count // PAGE_TOKENS
    page_rows = own_cols.reshape(page_count, PAGE_TOKENS, piece_cols)
    group_count = lax.axis_size("dp")
    capacity = page_count // group_count
    owners = page_table // page_count
    slot_ids = page_table % page_count
    hits = (owners[:, None] == jnp.arange(group_count, dtype=jnp.int32)[None, :]).astype(jnp.int32)
    order_in = jnp.sum((jnp.cumsum(hits, axis=0) - hits) * hits, axis=1)
    buffer_pos = owners * capacity + order_in
    source = (
        jnp.zeros((page_count,), jnp.int32)
        .at[buffer_pos]
        .set(jnp.arange(page_count, dtype=jnp.int32))
    )
    send_pages = page_rows[source].reshape(group_count, capacity, PAGE_TOKENS, piece_cols)
    send_slots = slot_ids[source].reshape(group_count, capacity)
    got_pages, got_slots = (
        lax.all_to_all(send_pages, "dp", split_axis=0, concat_axis=0, tiled=True),
        lax.all_to_all(send_slots, "dp", split_axis=0, concat_axis=0, tiled=True),
    )
    paged_key_value_cache = (
        jnp.zeros((page_count, PAGE_TOKENS, piece_cols), jnp.bfloat16)
        .at[got_slots.reshape(-1)]
        .set(got_pages.reshape(page_count, PAGE_TOKENS, piece_cols))
    )
    block_rows = min(512, token_count)
    block_total = token_count // block_rows
    score_scale = math.sqrt(HEAD_SIZE)
    all_ids = jnp.arange(token_count, dtype=jnp.int32)
    local_ids = jnp.arange(block_rows, dtype=jnp.int32)

    def dense_block(block_index):
        first_row = block_index * block_rows
        key_count = first_row + block_rows
        q_block = q_rot[first_row:key_count]
        q_prompt = prompt[first_row:key_count]
        row_ids = first_row + local_ids
        scores = (
            jnp.einsum(
                "qhd,kd->hqk", q_block, key_flat[:key_count], preferred_element_type=jnp.float32
            )
            / score_scale
        )
        allowed = (
            (q_prompt[:, None] == prompt[None, :key_count])
            & (row_ids[:, None] >= all_ids[None, :key_count])
        )[None]
        peak = jnp.max(jnp.where(allowed, scores, -jnp.inf), axis=2, keepdims=True)
        weight = jnp.where(allowed, jnp.exp(scores - peak), 0.0)
        total_weight = jnp.sum(weight, axis=2, keepdims=True)
        running = jnp.einsum(
            "hqk,kd->hqd",
            weight.astype(jnp.bfloat16),
            value_matrix_rows[:key_count],
            preferred_element_type=jnp.float32,
        )
        return (running / total_weight).astype(jnp.bfloat16)

    blocks_out = jnp.stack([dense_block(block_index) for block_index in range(block_total)])
    attn = jnp.transpose(blocks_out, (0, 2, 1, 3)).reshape(token_count, query_cols)
    attn_sum = scatter_sum(
        jnp.dot(attn, w_out, preferred_element_type=jnp.float32).astype(jnp.bfloat16),
        tensor_element_count,
    )
    resid = (stream.astype(jnp.float32) + attn_sum).astype(jnp.bfloat16)
    portion = gather_rows(row_norm(resid, mlp_gain).astype(jnp.bfloat16))
    paged_key_value_cache, portion = lax.optimization_barrier((paged_key_value_cache, portion))
    gate_rows = jnp.dot(portion, w_gate, preferred_element_type=jnp.float32)
    upward = jnp.dot(portion, w_up, preferred_element_type=jnp.float32)
    hidden = (jax.nn.silu(gate_rows) * upward).astype(jnp.bfloat16)
    width = w_down.shape[1]
    feat = width // tensor_element_count
    nprompt = prompt_ends.shape[0]
    end_pick = ((prompt_ends - 1)[:, None] == all_ids[None, :]).astype(jnp.bfloat16)
    end_hidden = jnp.dot(end_pick, hidden, preferred_element_type=jnp.float32).astype(jnp.bfloat16)
    end_down = jnp.dot(end_hidden, w_down, preferred_element_type=jnp.float32).astype(jnp.bfloat16)
    my_rows = my_index * tok_dev + jnp.arange(tok_dev, dtype=jnp.int32)
    select = ((prompt_ends - 1)[:, None] == my_rows[None, :]).astype(jnp.bfloat16)
    end_resid = jnp.dot(select, resid, preferred_element_type=jnp.float32).astype(jnp.bfloat16)

    def by_feature_block(rows):
        blocks = rows.reshape(nprompt, tensor_element_count, feat)
        return jnp.transpose(blocks, (1, 0, 2)).reshape(tensor_element_count, nprompt * feat)

    extra = jnp.concatenate([by_feature_block(end_down), by_feature_block(end_resid)], axis=1)
    extra_cols = 128
    extra = jnp.pad(extra, ((0, 0), (0, tok_dev * extra_cols - extra.shape[1])))
    wide_weight = jnp.concatenate(
        [w_down, jnp.zeros((w_down.shape[0], extra_cols), w_down.dtype)], axis=1
    )
    down = jnp.dot(hidden, wide_weight, preferred_element_type=jnp.float32).astype(jnp.bfloat16)
    payload = lax.dynamic_update_slice(
        down.reshape(tensor_element_count, tok_dev, width + extra_cols),
        extra.reshape(tensor_element_count, tok_dev, extra_cols),
        (0, 0, width),
    )
    got = lax.all_to_all(payload, TENSOR, 0, 0, tiled=True)
    summed = jnp.sum(got.astype(jnp.float32), axis=0)
    mlp_sum = summed[:, :width]
    layer_out = (resid.astype(jnp.float32) + mlp_sum).astype(jnp.bfloat16)
    tail = summed[:, width:].reshape(-1)
    end_rows = (
        (tail[: nprompt * feat] + tail[nprompt * feat : 2 * nprompt * feat])
        .reshape(nprompt, feat)
        .astype(jnp.bfloat16)
    )
    table = lax.all_gather(end_rows, "dp", axis=0, tiled=True)
    pick = (request_prompt[:, None] == jnp.arange(table.shape[0], dtype=jnp.int32)[None, :]).astype(
        jnp.bfloat16
    )
    request_state = jnp.dot(pick, table, preferred_element_type=jnp.float32).astype(jnp.bfloat16)
    return (layer_out, paged_key_value_cache, request_state)


def solution(mesh):
    placed = (
        P(("dp",) + TENSOR, None),
        P("dp", None),
        P("dp"),
        P("dp"),
        P(),
        P(),
        P(),
        P(),
        P(None, TENSOR),
        P(None, TENSOR),
        P(TENSOR, None),
        P(None, TENSOR),
        P(None, TENSOR),
        P(TENSOR, None),
    )
    dp_size = mesh.shape["dp"]
    fine = jax.sharding.Mesh(
        mesh.devices.reshape((dp_size,) + TENSOR_SHAPE), ("dp",) + TENSOR
    )
    return jax.shard_map(
        per_device,
        mesh=fine,
        in_specs=placed,
        out_specs=(P(("dp",) + TENSOR, None), P("dp", None, TENSOR), P("dp", TENSOR)),
        check_vma=False,
    )
```

```python
import math

import jax
import jax.numpy as jnp
from jax import lax
from jax.sharding import PartitionSpec as P

KEY_VALUE_HEADS = 8
HEAD_SIZE = 128
PAGE_TOKENS = 16
TENSOR = ("ty", "tx", "tz")
TENSOR_SHAPE = (4, 4, 2)


epsilon = 1e-06
rope_base = 1000000.0


def partner_2(value, axis, bit):
    mask = 2**bit
    pairs = [(source, source ^ mask) for source in range(lax.axis_size(axis))]
    return lax.ppermute(value, axis, pairs)


def scatter_sum(partial, parts):
    pieces = partial.reshape((parts, partial.shape[0] // parts) + partial.shape[1:])
    got = lax.all_to_all(pieces, TENSOR, 0, 0, tiled=True)
    return jnp.sum(got.astype(jnp.float32), axis=0)


def gather_rows(rows):
    rows = lax.all_gather(rows, "tz", axis=0, tiled=True)
    return lax.all_gather(rows, ("ty", "tx"), axis=0, tiled=True)


def row_norm(inputs, gain):
    inputs = inputs.astype(jnp.float32)
    scale = lax.rsqrt(jnp.mean(inputs * inputs, axis=-1, keepdims=True) + epsilon)
    return inputs * scale * gain.astype(jnp.float32)


def rotate(inputs, position):
    half_dim = inputs.shape[-1] // 2
    frequency = rope_base ** (-2.0 * jnp.arange(half_dim, dtype=jnp.float32) / inputs.shape[-1])
    angles = position.astype(jnp.float32)[:, None] * frequency[None, :]
    cosine = jnp.cos(angles)[:, None, :]
    sine_part = jnp.sin(angles)[:, None, :]
    front = inputs[..., :half_dim]
    second = inputs[..., half_dim:]
    return jnp.concatenate(
        [front * cosine - second * sine_part, second * cosine + front * sine_part], axis=-1
    )


def prompt_layout(lengths_row, token_count):
    prompt_ends = jnp.cumsum(lengths_row)
    prompt_starts = prompt_ends - lengths_row
    row_ids = jnp.arange(token_count, dtype=jnp.int32)
    prompt = jnp.sum((row_ids[:, None] >= prompt_ends[None, :]).astype(jnp.int32), axis=1)
    inside = (row_ids[:, None] >= prompt_starts[None, :]) & (
        row_ids[:, None] < prompt_ends[None, :]
    )
    offset = jnp.sum(jnp.where(inside, prompt_starts[None, :], 0), axis=1)
    return (prompt, row_ids - offset, prompt_starts, prompt_ends)


def per_device(
    stream,
    lengths,
    page_table,
    request_prompt,
    attn_gain,
    query_gain,
    key_gain,
    mlp_gain,
    w_query,
    key_value_weight,
    w_out,
    w_gate,
    w_up,
    w_down,
):
    tok_dev = stream.shape[0]
    tensor_element_count = lax.axis_size(TENSOR)
    token_count = tok_dev * tensor_element_count
    my_index = lax.axis_index(TENSOR)
    heads_dev = w_query.shape[1] // HEAD_SIZE
    query_cols = heads_dev * HEAD_SIZE
    prompt, position, prompt_starts, prompt_ends = prompt_layout(lengths[0], token_count)
    portion = gather_rows(row_norm(stream, attn_gain).astype(jnp.bfloat16))
    key_value_group = tensor_element_count // KEY_VALUE_HEADS
    head_weight = key_value_weight
    for bit_id in range(key_value_group.bit_length() - 1):
        partner = partner_2(head_weight, TENSOR, bit_id)
        upper_half = my_index // 2**bit_id % 2
        head_weight = jnp.where(
            upper_half == 1,
            jnp.concatenate([partner, head_weight], axis=1),
            jnp.concatenate([head_weight, partner], axis=1),
        )
    joined = jnp.dot(
        portion,
        jnp.concatenate([w_query, head_weight], axis=1),
        preferred_element_type=jnp.float32,
    )
    queries = joined[:, :query_cols].reshape(token_count, heads_dev, HEAD_SIZE)
    kv_part = joined[:, query_cols:].astype(jnp.bfloat16)
    key_flat = rotate(row_norm(kv_part[:, None, :HEAD_SIZE], key_gain), position).astype(
        jnp.bfloat16
    )[:, 0, :]
    value_matrix_rows = kv_part[:, HEAD_SIZE:]
    q_rot = rotate(row_norm(queries, query_gain), position).astype(jnp.bfloat16)
    piece_cols = key_value_weight.shape[1]
    head_rows = jnp.concatenate([key_flat, value_matrix_rows], axis=1)
    own_cols = lax.dynamic_slice_in_dim(
        head_rows, my_index % key_value_group * piece_cols, piece_cols, 1
    )
    page_count = token_count // PAGE_TOKENS
    page_rows = own_cols.reshape(page_count, PAGE_TOKENS, piece_cols)
    group_count = lax.axis_size("dp")
    capacity = page_count // group_count
    owners = page_table // page_count
    slot_ids = page_table % page_count
    hits = (owners[:, None] == jnp.arange(group_count, dtype=jnp.int32)[None, :]).astype(jnp.int32)
    order_in = jnp.sum((jnp.cumsum(hits, axis=0) - hits) * hits, axis=1)
    buffer_pos = owners * capacity + order_in
    source = (
        jnp.zeros((page_count,), jnp.int32)
        .at[buffer_pos]
        .set(jnp.arange(page_count, dtype=jnp.int32))
    )
    send_pages = page_rows[source].reshape(group_count, capacity, PAGE_TOKENS, piece_cols)
    send_slots = slot_ids[source].reshape(group_count, capacity)
    got_pages, got_slots = (
        lax.all_to_all(send_pages, "dp", split_axis=0, concat_axis=0, tiled=True),
        lax.all_to_all(send_slots, "dp", split_axis=0, concat_axis=0, tiled=True),
    )
    paged_key_value_cache = (
        jnp.zeros((page_count, PAGE_TOKENS, piece_cols), jnp.bfloat16)
        .at[got_slots.reshape(-1)]
        .set(got_pages.reshape(page_count, PAGE_TOKENS, piece_cols))
    )
    block_rows = min(512, token_count)
    block_total = token_count // block_rows
    score_scale = math.sqrt(HEAD_SIZE)
    all_ids = jnp.arange(token_count, dtype=jnp.int32)
    local_ids = jnp.arange(block_rows, dtype=jnp.int32)

    def dense_block(block_index):
        first_row = block_index * block_rows
        key_count = first_row + block_rows
        q_block = q_rot[first_row:key_count]
        q_prompt = prompt[first_row:key_count]
        row_ids = first_row + local_ids
        scores = (
            jnp.einsum(
                "qhd,kd->hqk", q_block, key_flat[:key_count], preferred_element_type=jnp.float32
            )
            / score_scale
        )
        allowed = (
            (q_prompt[:, None] == prompt[None, :key_count])
            & (row_ids[:, None] >= all_ids[None, :key_count])
        )[None]
        peak = jnp.max(jnp.where(allowed, scores, -jnp.inf), axis=2, keepdims=True)
        weight = jnp.where(allowed, jnp.exp(scores - peak), 0.0)
        total_weight = jnp.sum(weight, axis=2, keepdims=True)
        running = jnp.einsum(
            "hqk,kd->hqd",
            weight.astype(jnp.bfloat16),
            value_matrix_rows[:key_count],
            preferred_element_type=jnp.float32,
        )
        return (running / total_weight).astype(jnp.bfloat16)

    blocks_out = jnp.stack([dense_block(block_index) for block_index in range(block_total)])
    attn = jnp.transpose(blocks_out, (0, 2, 1, 3)).reshape(token_count, query_cols)
    attn_sum = scatter_sum(
        jnp.dot(attn, w_out, preferred_element_type=jnp.float32).astype(jnp.bfloat16),
        tensor_element_count,
    )
    resid = (stream.astype(jnp.float32) + attn_sum).astype(jnp.bfloat16)
    portion = gather_rows(row_norm(resid, mlp_gain).astype(jnp.bfloat16))
    paged_key_value_cache, portion = lax.optimization_barrier((paged_key_value_cache, portion))
    gate_rows = jnp.dot(portion, w_gate, preferred_element_type=jnp.float32)
    upward = jnp.dot(portion, w_up, preferred_element_type=jnp.float32)
    hidden = (jax.nn.silu(gate_rows) * upward).astype(jnp.bfloat16)
    width = w_down.shape[1]
    feat = width // tensor_element_count
    nprompt = prompt_ends.shape[0]
    end_pick = ((prompt_ends - 1)[:, None] == all_ids[None, :]).astype(jnp.bfloat16)
    end_hidden = jnp.dot(end_pick, hidden, preferred_element_type=jnp.float32).astype(jnp.bfloat16)
    end_down = jnp.dot(end_hidden, w_down, preferred_element_type=jnp.float32).astype(jnp.bfloat16)
    my_rows = my_index * tok_dev + jnp.arange(tok_dev, dtype=jnp.int32)
    select = ((prompt_ends - 1)[:, None] == my_rows[None, :]).astype(jnp.bfloat16)
    end_resid = jnp.dot(select, resid, preferred_element_type=jnp.float32).astype(jnp.bfloat16)

    def by_feature_block(rows):
        blocks = rows.reshape(nprompt, tensor_element_count, feat)
        return jnp.transpose(blocks, (1, 0, 2)).reshape(tensor_element_count, nprompt * feat)

    extra = jnp.concatenate([by_feature_block(end_down), by_feature_block(end_resid)], axis=1)
    extra_cols = 128
    extra = jnp.pad(extra, ((0, 0), (0, tok_dev * extra_cols - extra.shape[1])))
    wide_weight = jnp.concatenate(
        [w_down, jnp.zeros((w_down.shape[0], extra_cols), w_down.dtype)], axis=1
    )
    down = jnp.dot(hidden, wide_weight, preferred_element_type=jnp.float32).astype(jnp.bfloat16)
    payload = lax.dynamic_update_slice(
        down.reshape(tensor_element_count, tok_dev, width + extra_cols),
        extra.reshape(tensor_element_count, tok_dev, extra_cols),
        (0, 0, width),
    )
    got = lax.all_to_all(payload, TENSOR, 0, 0, tiled=True)
    summed = jnp.sum(got.astype(jnp.float32), axis=0)
    mlp_sum = summed[:, :width]
    layer_out = (resid.astype(jnp.float32) + mlp_sum).astype(jnp.bfloat16)
    tail = summed[:, width:].reshape(-1)
    end_rows = (
        (tail[: nprompt * feat] + tail[nprompt * feat : 2 * nprompt * feat])
        .reshape(nprompt, feat)
        .astype(jnp.bfloat16)
    )
    table = lax.all_gather(end_rows, "dp", axis=0, tiled=True)
    pick = (request_prompt[:, None] == jnp.arange(table.shape[0], dtype=jnp.int32)[None, :]).astype(
        jnp.bfloat16
    )
    request_state = jnp.dot(pick, table, preferred_element_type=jnp.float32).astype(jnp.bfloat16)
    return (layer_out, paged_key_value_cache, request_state)


def solution(mesh):
    placed = (
        P(("dp",) + TENSOR, None),
        P("dp", None),
        P("dp"),
        P("dp"),
        P(),
        P(),
        P(),
        P(),
        P(None, TENSOR),
        P(None, TENSOR),
        P(TENSOR, None),
        P(None, TENSOR),
        P(None, TENSOR),
        P(TENSOR, None),
    )
    dp_size = mesh.shape["dp"]
    fine = jax.sharding.Mesh(
        mesh.devices.reshape((dp_size,) + TENSOR_SHAPE), ("dp",) + TENSOR
    )
    return jax.shard_map(
        per_device,
        mesh=fine,
        in_specs=placed,
        out_specs=(P(("dp",) + TENSOR, None), P("dp", None, TENSOR), P("dp", TENSOR)),
        check_vma=False,
    )
```

```python
import math

import jax
import jax.numpy as jnp
from jax import lax
from jax.sharding import PartitionSpec as P

KEY_VALUE_HEADS = 8
HEAD_SIZE = 128
PAGE_TOKENS = 16
TENSOR = ("ty", "tx", "tz")
TENSOR_SHAPE = (4, 4, 2)


epsilon = 1e-06
rope_base = 1000000.0


def partner_2(value, axis, bit):
    mask = 2**bit
    pairs = [(source, source ^ mask) for source in range(lax.axis_size(axis))]
    return lax.ppermute(value, axis, pairs)


def scatter_sum(partial, parts):
    pieces = partial.reshape((parts, partial.shape[0] // parts) + partial.shape[1:])
    got = lax.all_to_all(pieces, TENSOR, 0, 0, tiled=True)
    return jnp.sum(got.astype(jnp.float32), axis=0)


def gather_rows(rows):
    rows = lax.all_gather(rows, "tz", axis=0, tiled=True)
    return lax.all_gather(rows, ("ty", "tx"), axis=0, tiled=True)


def row_norm(inputs, gain):
    inputs = inputs.astype(jnp.float32)
    scale = lax.rsqrt(jnp.mean(inputs * inputs, axis=-1, keepdims=True) + epsilon)
    return inputs * scale * gain.astype(jnp.float32)


def rotate(inputs, position):
    half_dim = inputs.shape[-1] // 2
    frequency = rope_base ** (-2.0 * jnp.arange(half_dim, dtype=jnp.float32) / inputs.shape[-1])
    angles = position.astype(jnp.float32)[:, None] * frequency[None, :]
    cosine = jnp.cos(angles)[:, None, :]
    sine_part = jnp.sin(angles)[:, None, :]
    front = inputs[..., :half_dim]
    second = inputs[..., half_dim:]
    return jnp.concatenate(
        [front * cosine - second * sine_part, second * cosine + front * sine_part], axis=-1
    )


def prompt_layout(lengths_row, token_count):
    prompt_ends = jnp.cumsum(lengths_row)
    prompt_starts = prompt_ends - lengths_row
    row_ids = jnp.arange(token_count, dtype=jnp.int32)
    prompt = jnp.sum((row_ids[:, None] >= prompt_ends[None, :]).astype(jnp.int32), axis=1)
    inside = (row_ids[:, None] >= prompt_starts[None, :]) & (
        row_ids[:, None] < prompt_ends[None, :]
    )
    offset = jnp.sum(jnp.where(inside, prompt_starts[None, :], 0), axis=1)
    return (prompt, row_ids - offset, prompt_starts, prompt_ends)


def per_device(
    stream,
    lengths,
    page_table,
    request_prompt,
    attn_gain,
    query_gain,
    key_gain,
    mlp_gain,
    w_query,
    key_value_weight,
    w_out,
    w_gate,
    w_up,
    w_down,
):
    tok_dev = stream.shape[0]
    tensor_element_count = lax.axis_size(TENSOR)
    token_count = tok_dev * tensor_element_count
    my_index = lax.axis_index(TENSOR)
    heads_dev = w_query.shape[1] // HEAD_SIZE
    query_cols = heads_dev * HEAD_SIZE
    prompt, position, prompt_starts, prompt_ends = prompt_layout(lengths[0], token_count)
    portion = gather_rows(row_norm(stream, attn_gain).astype(jnp.bfloat16))
    key_value_group = tensor_element_count // KEY_VALUE_HEADS
    head_weight = key_value_weight
    for bit_id in range(key_value_group.bit_length() - 1):
        partner = partner_2(head_weight, TENSOR, bit_id)
        upper_half = my_index // 2**bit_id % 2
        head_weight = jnp.where(
            upper_half == 1,
            jnp.concatenate([partner, head_weight], axis=1),
            jnp.concatenate([head_weight, partner], axis=1),
        )
    joined = jnp.dot(
        portion,
        jnp.concatenate([w_query, head_weight], axis=1),
        preferred_element_type=jnp.float32,
    )
    queries = joined[:, :query_cols].reshape(token_count, heads_dev, HEAD_SIZE)
    kv_part = joined[:, query_cols:].astype(jnp.bfloat16)
    key_flat = rotate(row_norm(kv_part[:, None, :HEAD_SIZE], key_gain), position).astype(
        jnp.bfloat16
    )[:, 0, :]
    value_matrix_rows = kv_part[:, HEAD_SIZE:]
    q_rot = rotate(row_norm(queries, query_gain), position).astype(jnp.bfloat16)
    piece_cols = key_value_weight.shape[1]
    head_rows = jnp.concatenate([key_flat, value_matrix_rows], axis=1)
    own_cols = lax.dynamic_slice_in_dim(
        head_rows, my_index % key_value_group * piece_cols, piece_cols, 1
    )
    page_count = token_count // PAGE_TOKENS
    page_rows = own_cols.reshape(page_count, PAGE_TOKENS, piece_cols)
    group_count = lax.axis_size("dp")
    capacity = page_count // group_count
    owners = page_table // page_count
    slot_ids = page_table % page_count
    hits = (owners[:, None] == jnp.arange(group_count, dtype=jnp.int32)[None, :]).astype(jnp.int32)
    order_in = jnp.sum((jnp.cumsum(hits, axis=0) - hits) * hits, axis=1)
    buffer_pos = owners * capacity + order_in
    source = (
        jnp.zeros((page_count,), jnp.int32)
        .at[buffer_pos]
        .set(jnp.arange(page_count, dtype=jnp.int32))
    )
    send_pages = page_rows[source].reshape(group_count, capacity, PAGE_TOKENS, piece_cols)
    send_slots = slot_ids[source].reshape(group_count, capacity)
    got_pages, got_slots = (
        lax.all_to_all(send_pages, "dp", split_axis=0, concat_axis=0, tiled=True),
        lax.all_to_all(send_slots, "dp", split_axis=0, concat_axis=0, tiled=True),
    )
    paged_key_value_cache = (
        jnp.zeros((page_count, PAGE_TOKENS, piece_cols), jnp.bfloat16)
        .at[got_slots.reshape(-1)]
        .set(got_pages.reshape(page_count, PAGE_TOKENS, piece_cols))
    )
    block_rows = min(512, token_count)
    block_total = token_count // block_rows
    score_scale = math.sqrt(HEAD_SIZE)
    all_ids = jnp.arange(token_count, dtype=jnp.int32)
    local_ids = jnp.arange(block_rows, dtype=jnp.int32)

    def dense_block(block_index):
        first_row = block_index * block_rows
        key_count = first_row + block_rows
        q_block = q_rot[first_row:key_count]
        q_prompt = prompt[first_row:key_count]
        row_ids = first_row + local_ids
        scores = (
            jnp.einsum(
                "qhd,kd->hqk", q_block, key_flat[:key_count], preferred_element_type=jnp.float32
            )
            / score_scale
        )
        allowed = (
            (q_prompt[:, None] == prompt[None, :key_count])
            & (row_ids[:, None] >= all_ids[None, :key_count])
        )[None]
        peak = jnp.max(jnp.where(allowed, scores, -jnp.inf), axis=2, keepdims=True)
        weight = jnp.where(allowed, jnp.exp(scores - peak), 0.0)
        total_weight = jnp.sum(weight, axis=2, keepdims=True)
        running = jnp.einsum(
            "hqk,kd->hqd",
            weight.astype(jnp.bfloat16),
            value_matrix_rows[:key_count],
            preferred_element_type=jnp.float32,
        )
        return (running / total_weight).astype(jnp.bfloat16)

    blocks_out = jnp.stack([dense_block(block_index) for block_index in range(block_total)])
    attn = jnp.transpose(blocks_out, (0, 2, 1, 3)).reshape(token_count, query_cols)
    attn_sum = scatter_sum(
        jnp.dot(attn, w_out, preferred_element_type=jnp.float32).astype(jnp.bfloat16),
        tensor_element_count,
    )
    resid = (stream.astype(jnp.float32) + attn_sum).astype(jnp.bfloat16)
    portion = gather_rows(row_norm(resid, mlp_gain).astype(jnp.bfloat16))
    paged_key_value_cache, portion = lax.optimization_barrier((paged_key_value_cache, portion))
    both = jnp.dot(
        portion, jnp.concatenate([w_gate, w_up], axis=1), preferred_element_type=jnp.float32
    )
    gate_rows = both[:, : w_gate.shape[1]]
    upward = both[:, w_gate.shape[1] :]
    hidden = (jax.nn.silu(gate_rows) * upward).astype(jnp.bfloat16)
    width = w_down.shape[1]
    feat = width // tensor_element_count
    nprompt = prompt_ends.shape[0]
    end_pick = ((prompt_ends - 1)[:, None] == all_ids[None, :]).astype(jnp.bfloat16)
    end_hidden = jnp.dot(end_pick, hidden, preferred_element_type=jnp.float32).astype(jnp.bfloat16)
    end_down = jnp.dot(end_hidden, w_down, preferred_element_type=jnp.float32).astype(jnp.bfloat16)
    my_rows = my_index * tok_dev + jnp.arange(tok_dev, dtype=jnp.int32)
    select = ((prompt_ends - 1)[:, None] == my_rows[None, :]).astype(jnp.bfloat16)
    end_resid = jnp.dot(select, resid, preferred_element_type=jnp.float32).astype(jnp.bfloat16)

    def by_feature_block(rows):
        blocks = rows.reshape(nprompt, tensor_element_count, feat)
        return jnp.transpose(blocks, (1, 0, 2)).reshape(tensor_element_count, nprompt * feat)

    extra = jnp.concatenate([by_feature_block(end_down), by_feature_block(end_resid)], axis=1)
    extra_cols = 128
    extra = jnp.pad(extra, ((0, 0), (0, tok_dev * extra_cols - extra.shape[1])))
    wide_weight = jnp.concatenate(
        [w_down, jnp.zeros((w_down.shape[0], extra_cols), w_down.dtype)], axis=1
    )
    down = jnp.dot(hidden, wide_weight, preferred_element_type=jnp.float32).astype(jnp.bfloat16)
    payload = lax.dynamic_update_slice(
        down.reshape(tensor_element_count, tok_dev, width + extra_cols),
        extra.reshape(tensor_element_count, tok_dev, extra_cols),
        (0, 0, width),
    )
    got = lax.all_to_all(payload, TENSOR, 0, 0, tiled=True)
    summed = jnp.sum(got.astype(jnp.float32), axis=0)
    mlp_sum = summed[:, :width]
    layer_out = (resid.astype(jnp.float32) + mlp_sum).astype(jnp.bfloat16)
    tail = summed[:, width:].reshape(-1)
    end_rows = (
        (tail[: nprompt * feat] + tail[nprompt * feat : 2 * nprompt * feat])
        .reshape(nprompt, feat)
        .astype(jnp.bfloat16)
    )
    table = lax.all_gather(end_rows, "dp", axis=0, tiled=True)
    pick = (request_prompt[:, None] == jnp.arange(table.shape[0], dtype=jnp.int32)[None, :]).astype(
        jnp.bfloat16
    )
    request_state = jnp.dot(pick, table, preferred_element_type=jnp.float32).astype(jnp.bfloat16)
    return (layer_out, paged_key_value_cache, request_state)


def solution(mesh):
    placed = (
        P(("dp",) + TENSOR, None),
        P("dp", None),
        P("dp"),
        P("dp"),
        P(),
        P(),
        P(),
        P(),
        P(None, TENSOR),
        P(None, TENSOR),
        P(TENSOR, None),
        P(None, TENSOR),
        P(None, TENSOR),
        P(TENSOR, None),
    )
    dp_size = mesh.shape["dp"]
    fine = jax.sharding.Mesh(
        mesh.devices.reshape((dp_size,) + TENSOR_SHAPE), ("dp",) + TENSOR
    )
    return jax.shard_map(
        per_device,
        mesh=fine,
        in_specs=placed,
        out_specs=(P(("dp",) + TENSOR, None), P("dp", None, TENSOR), P("dp", TENSOR)),
        check_vma=False,
    )
```

```python
import math

import jax
import jax.numpy as jnp
from jax import lax
from jax.sharding import PartitionSpec as P

KEY_VALUE_HEADS = 8
HEAD_SIZE = 128
PAGE_TOKENS = 16
TENSOR = ("ty", "tx", "tz")
TENSOR_SHAPE = (4, 4, 2)


epsilon = 1e-06
rope_base = 1000000.0


def partner_2(value, axis, bit):
    mask = 2**bit
    pairs = [(source, source ^ mask) for source in range(lax.axis_size(axis))]
    return lax.ppermute(value, axis, pairs)


def scatter_sum(partial, parts):
    pieces = partial.reshape((parts, partial.shape[0] // parts) + partial.shape[1:])
    got = lax.all_to_all(pieces, TENSOR, 0, 0, tiled=True)
    return jnp.sum(got.astype(jnp.float32), axis=0)


def gather_rows(rows):
    rows = lax.all_gather(rows, "tz", axis=0, tiled=True)
    return lax.all_gather(rows, ("ty", "tx"), axis=0, tiled=True)


def row_norm(inputs, gain):
    inputs = inputs.astype(jnp.float32)
    scale = lax.rsqrt(jnp.mean(inputs * inputs, axis=-1, keepdims=True) + epsilon)
    return inputs * scale * gain.astype(jnp.float32)


def rotate(inputs, position):
    half_dim = inputs.shape[-1] // 2
    frequency = rope_base ** (-2.0 * jnp.arange(half_dim, dtype=jnp.float32) / inputs.shape[-1])
    angles = position.astype(jnp.float32)[:, None] * frequency[None, :]
    cosine = jnp.cos(angles)[:, None, :]
    sine_part = jnp.sin(angles)[:, None, :]
    front = inputs[..., :half_dim]
    second = inputs[..., half_dim:]
    return jnp.concatenate(
        [front * cosine - second * sine_part, second * cosine + front * sine_part], axis=-1
    )


def prompt_layout(lengths_row, token_count):
    prompt_ends = jnp.cumsum(lengths_row)
    prompt_starts = prompt_ends - lengths_row
    row_ids = jnp.arange(token_count, dtype=jnp.int32)
    prompt = jnp.sum((row_ids[:, None] >= prompt_ends[None, :]).astype(jnp.int32), axis=1)
    inside = (row_ids[:, None] >= prompt_starts[None, :]) & (
        row_ids[:, None] < prompt_ends[None, :]
    )
    offset = jnp.sum(jnp.where(inside, prompt_starts[None, :], 0), axis=1)
    return (prompt, row_ids - offset, prompt_starts, prompt_ends)


def per_device(
    stream,
    lengths,
    page_table,
    request_prompt,
    attn_gain,
    query_gain,
    key_gain,
    mlp_gain,
    w_query,
    key_value_weight,
    w_out,
    w_gate,
    w_up,
    w_down,
):
    tok_dev = stream.shape[0]
    tensor_element_count = lax.axis_size(TENSOR)
    token_count = tok_dev * tensor_element_count
    my_index = lax.axis_index(TENSOR)
    heads_dev = w_query.shape[1] // HEAD_SIZE
    query_cols = heads_dev * HEAD_SIZE
    prompt, position, prompt_starts, prompt_ends = prompt_layout(lengths[0], token_count)
    portion = gather_rows(row_norm(stream, attn_gain).astype(jnp.bfloat16))
    key_value_group = tensor_element_count // KEY_VALUE_HEADS
    head_weight = key_value_weight
    for bit_id in range(key_value_group.bit_length() - 1):
        partner = partner_2(head_weight, TENSOR, bit_id)
        upper_half = my_index // 2**bit_id % 2
        head_weight = jnp.where(
            upper_half == 1,
            jnp.concatenate([partner, head_weight], axis=1),
            jnp.concatenate([head_weight, partner], axis=1),
        )
    joined = jnp.dot(
        portion,
        jnp.concatenate([w_query, head_weight], axis=1),
        preferred_element_type=jnp.float32,
    )
    queries = joined[:, :query_cols].reshape(token_count, heads_dev, HEAD_SIZE)
    kv_part = joined[:, query_cols:].astype(jnp.bfloat16)
    key_flat = rotate(row_norm(kv_part[:, None, :HEAD_SIZE], key_gain), position).astype(
        jnp.bfloat16
    )[:, 0, :]
    value_matrix_rows = kv_part[:, HEAD_SIZE:]
    q_rot = rotate(row_norm(queries, query_gain), position).astype(jnp.bfloat16)
    piece_cols = key_value_weight.shape[1]
    head_rows = jnp.concatenate([key_flat, value_matrix_rows], axis=1)
    own_cols = lax.dynamic_slice_in_dim(
        head_rows, my_index % key_value_group * piece_cols, piece_cols, 1
    )
    page_count = token_count // PAGE_TOKENS
    page_rows = own_cols.reshape(page_count, PAGE_TOKENS, piece_cols)
    group_count = lax.axis_size("dp")
    capacity = page_count // group_count
    owners = page_table // page_count
    slot_ids = page_table % page_count
    hits = (owners[:, None] == jnp.arange(group_count, dtype=jnp.int32)[None, :]).astype(jnp.int32)
    order_in = jnp.sum((jnp.cumsum(hits, axis=0) - hits) * hits, axis=1)
    buffer_pos = owners * capacity + order_in
    source = (
        jnp.zeros((page_count,), jnp.int32)
        .at[buffer_pos]
        .set(jnp.arange(page_count, dtype=jnp.int32))
    )
    send_pages = page_rows[source].reshape(group_count, capacity, PAGE_TOKENS, piece_cols)
    send_slots = slot_ids[source].reshape(group_count, capacity)
    got_pages, got_slots = (
        lax.all_to_all(send_pages, "dp", split_axis=0, concat_axis=0, tiled=True),
        lax.all_to_all(send_slots, "dp", split_axis=0, concat_axis=0, tiled=True),
    )
    paged_key_value_cache = (
        jnp.zeros((page_count, PAGE_TOKENS, piece_cols), jnp.bfloat16)
        .at[got_slots.reshape(-1)]
        .set(got_pages.reshape(page_count, PAGE_TOKENS, piece_cols))
    )
    block_rows = min(512, token_count)
    block_total = token_count // block_rows
    score_scale = math.sqrt(HEAD_SIZE)
    all_ids = jnp.arange(token_count, dtype=jnp.int32)
    local_ids = jnp.arange(block_rows, dtype=jnp.int32)

    def dense_block(block_index):
        first_row = block_index * block_rows
        key_count = first_row + block_rows
        key_first = max(0, first_row - 768)
        q_block = q_rot[first_row:key_count]
        q_prompt = prompt[first_row:key_count]
        row_ids = first_row + local_ids
        scores = (
            jnp.einsum(
                "qhd,kd->hqk",
                q_block,
                key_flat[key_first:key_count],
                preferred_element_type=jnp.float32,
            )
            / score_scale
        )
        allowed = (
            (q_prompt[:, None] == prompt[None, key_first:key_count])
            & (row_ids[:, None] >= all_ids[None, key_first:key_count])
        )[None]
        peak = jnp.max(jnp.where(allowed, scores, -jnp.inf), axis=2, keepdims=True)
        weight = jnp.where(allowed, jnp.exp(scores - peak), 0.0)
        total_weight = jnp.sum(weight, axis=2, keepdims=True)
        running = jnp.einsum(
            "hqk,kd->hqd",
            weight.astype(jnp.bfloat16),
            value_matrix_rows[key_first:key_count],
            preferred_element_type=jnp.float32,
        )
        return (running / total_weight).astype(jnp.bfloat16)

    blocks_out = jnp.stack([dense_block(block_index) for block_index in range(block_total)])
    attn = jnp.transpose(blocks_out, (0, 2, 1, 3)).reshape(token_count, query_cols)
    attn_sum = scatter_sum(
        jnp.dot(attn, w_out, preferred_element_type=jnp.float32).astype(jnp.bfloat16),
        tensor_element_count,
    )
    resid = (stream.astype(jnp.float32) + attn_sum).astype(jnp.bfloat16)
    portion = gather_rows(row_norm(resid, mlp_gain).astype(jnp.bfloat16))
    paged_key_value_cache, portion = lax.optimization_barrier((paged_key_value_cache, portion))
    both = jnp.dot(
        portion, jnp.concatenate([w_gate, w_up], axis=1), preferred_element_type=jnp.float32
    )
    gate_rows = both[:, : w_gate.shape[1]]
    upward = both[:, w_gate.shape[1] :]
    hidden = (jax.nn.silu(gate_rows) * upward).astype(jnp.bfloat16)
    width = w_down.shape[1]
    feat = width // tensor_element_count
    nprompt = prompt_ends.shape[0]
    end_pick = ((prompt_ends - 1)[:, None] == all_ids[None, :]).astype(jnp.bfloat16)
    end_hidden = jnp.dot(end_pick, hidden, preferred_element_type=jnp.float32).astype(jnp.bfloat16)
    end_down = jnp.dot(end_hidden, w_down, preferred_element_type=jnp.float32).astype(jnp.bfloat16)
    my_rows = my_index * tok_dev + jnp.arange(tok_dev, dtype=jnp.int32)
    select = ((prompt_ends - 1)[:, None] == my_rows[None, :]).astype(jnp.bfloat16)
    end_resid = jnp.dot(select, resid, preferred_element_type=jnp.float32).astype(jnp.bfloat16)

    def by_feature_block(rows):
        blocks = rows.reshape(nprompt, tensor_element_count, feat)
        return jnp.transpose(blocks, (1, 0, 2)).reshape(tensor_element_count, nprompt * feat)

    extra = jnp.concatenate([by_feature_block(end_down), by_feature_block(end_resid)], axis=1)
    extra_cols = 128
    extra = jnp.pad(extra, ((0, 0), (0, tok_dev * extra_cols - extra.shape[1])))
    wide_weight = jnp.concatenate(
        [w_down, jnp.zeros((w_down.shape[0], extra_cols), w_down.dtype)], axis=1
    )
    down = jnp.dot(hidden, wide_weight, preferred_element_type=jnp.float32).astype(jnp.bfloat16)
    payload = lax.dynamic_update_slice(
        down.reshape(tensor_element_count, tok_dev, width + extra_cols),
        extra.reshape(tensor_element_count, tok_dev, extra_cols),
        (0, 0, width),
    )
    got = lax.all_to_all(payload, TENSOR, 0, 0, tiled=True)
    summed = jnp.sum(got.astype(jnp.float32), axis=0)
    mlp_sum = summed[:, :width]
    layer_out = (resid.astype(jnp.float32) + mlp_sum).astype(jnp.bfloat16)
    tail = summed[:, width:].reshape(-1)
    end_rows = (
        (tail[: nprompt * feat] + tail[nprompt * feat : 2 * nprompt * feat])
        .reshape(nprompt, feat)
        .astype(jnp.bfloat16)
    )
    table = lax.all_gather(end_rows, "dp", axis=0, tiled=True)
    pick = (request_prompt[:, None] == jnp.arange(table.shape[0], dtype=jnp.int32)[None, :]).astype(
        jnp.bfloat16
    )
    request_state = jnp.dot(pick, table, preferred_element_type=jnp.float32).astype(jnp.bfloat16)
    return (layer_out, paged_key_value_cache, request_state)


def solution(mesh):
    placed = (
        P(("dp",) + TENSOR, None),
        P("dp", None),
        P("dp"),
        P("dp"),
        P(),
        P(),
        P(),
        P(),
        P(None, TENSOR),
        P(None, TENSOR),
        P(TENSOR, None),
        P(None, TENSOR),
        P(None, TENSOR),
        P(TENSOR, None),
    )
    dp_size = mesh.shape["dp"]
    fine = jax.sharding.Mesh(
        mesh.devices.reshape((dp_size,) + TENSOR_SHAPE), ("dp",) + TENSOR
    )
    return jax.shard_map(
        per_device,
        mesh=fine,
        in_specs=placed,
        out_specs=(P(("dp",) + TENSOR, None), P("dp", None, TENSOR), P("dp", TENSOR)),
        check_vma=False,
    )
```
